256 devices in a mesh: phase: 2 (over core), seq: 16 (over y_hi, z), dp: 8 (over x, y_lo).
Axes of the slice: x: 4, y: 4 (y_hi: 2, y_lo: 2; y = y_hi * 2 + y_lo), z: 8, core: 2. Of those that a mesh axis runs over, the one named last changes fastest.
Arguments:
- sections: bfloat16 [2, 2, 16384, 2048], P('phase', None, ('dp', 'seq')), may hold values from -6 to 6
- head_gains: float32 [2, 32], replicated, may hold values from 1 to 2
- block_counts: int32 [8, 2, 8], P('dp'), may hold values from 1 to 4, as said below
Outputs:
- result: bfloat16 [2, 2, 16384, 2048], P('phase', None, ('dp', 'seq'))
- gain_grads: float32 [2, 32], P('phase')
The draws below stay inside these ranges and needn't reach their ends.
Inputs may be any that keep to these rules, and one draw needn't show every extreme that they name: In every batch group both rows of block_counts sum to 16; decoder counts are at most 3 and encoder counts at most 4, both reached in every group; at every segment's start the encoder block offset exceeds the decoder block offset by 0 or 1.
All inputs are finite; a program needn't handle non-finite values.
Results may differ from the reference program's by a relative error of at most 0.013.
The reference program's roundings to bfloat16 on the way count: a program that leaves them out, or rounds other values in their place, can miss the bound.
Values may be sent and summed in bfloat16 or wider, within the bound.
No kernel may reach another device: no remote copies, remote signals or barrier semaphores. Data moves between devices by JAX's collectives and lax.ppermute only.
A program may use at most 128 MiB of HBM per device.

```python
import math
import jax
import jax.numpy as jnp
from jax import lax

H = 32
HD = 64
BLOCK = 128
ENC_MOST = 4
BLK_DEV = 1
INNER = 2048
NSEG = 8
GROUPS = 8
TOKENS = 16384
N_SEQ = 16
N_DP = 8


def draw_sections(key, part):
    full_shape = (2, 2, TOKENS, INNER)
    first_key = jax.random.fold_in(key, 0)
    values = jax.random.truncated_normal(first_key, -6.0, 6.0, full_shape, jnp.float32)
    return values.astype(jnp.bfloat16)


def draw_block_counts(key, part):

    def one_group(group_key):
        pick_key, order_key, place_key, coin_key = jax.random.split(group_key, 4)
        pair_total = (NSEG - 4) // 2
        pair_shift = jax.random.randint(pick_key, (pair_total,), -1, 2).astype(jnp.int32)
        paired = jnp.stack([2 + pair_shift, 2 - pair_shift], axis=1).reshape(-1).astype(jnp.int32)
        remainder = jax.random.permutation(order_key, jnp.concatenate([jnp.array([1, 2], jnp.int32), paired]))
        insert_at = jax.random.randint(place_key, (), 0, NSEG - 1).astype(jnp.int32)
        slots = jnp.arange(NSEG, dtype=jnp.int32)
        before = remainder[jnp.clip(slots, 0, NSEG - 3)]
        later_part = remainder[jnp.clip(slots - 2, 0, NSEG - 3)]
        decoder = jnp.where(slots < insert_at, before, jnp.where(slots == insert_at, 3, jnp.where(slots == insert_at + 1, 2, later_part)))
        boundary = jnp.arange(NSEG + 1, dtype=jnp.int32)
        coin_flips = jax.random.randint(coin_key, (NSEG + 1,), 0, 2).astype(jnp.int32)
        at_least_two = jnp.concatenate([decoder, jnp.zeros((1,), jnp.int32)]) >= 2
        interior = jnp.logical_and(boundary >= 1, boundary <= NSEG - 1)
        offsets = jnp.where(jnp.logical_and(interior, at_least_two), coin_flips, 0)
        offsets = jnp.where(boundary == insert_at, 0, offsets)
        offsets = jnp.where(boundary == insert_at + 1, 1, offsets)
        encoder = decoder + offsets[1:] - offsets[:-1]
        return jnp.stack([encoder, decoder]).astype(jnp.int32)
    group_keys = jax.random.split(key, GROUPS)
    return jax.vmap(one_group)(group_keys)


def setup_inputs(seed: int = 0) -> dict:
    arg_keys = jax.random.split(jax.random.key(seed), 4)
    sections = draw_sections(jax.random.fold_in(arg_keys[3], 71), 0)
    head_gains = jnp.clip(jnp.exp(jax.random.uniform(arg_keys[1], (2, H), jnp.float32, math.log(1.0), math.log(2.0))), 1.0, 2.0)
    block_counts = draw_block_counts(jax.random.fold_in(arg_keys[3], 71), 0)
    return {"sections": sections, "head_gains": head_gains, "block_counts": block_counts}


masked_score = -1e+30

def segment_of(block_ids, block_sizes, block_total):
    starts = (jnp.cumsum(block_sizes) - block_sizes).astype(jnp.int32)
    found = lax.optimization_barrier(jnp.sum((starts[None, :] <= block_ids[:, None]).astype(jnp.int32), axis=1)).astype(jnp.int32) - 1
    inside = jnp.logical_and(block_ids >= 0, block_ids < block_total)
    return jnp.where(inside, found, -1).astype(jnp.int32)

def cross_tile(queries, upstream, key_rows, value_rows, allowed, gain_logit, gain_value):
    row_count = queries.shape[0]
    key_count = key_rows.shape[0]
    head_count = gain_logit.shape[0]
    head_size = queries.shape[1] // head_count
    inv_root = 1.0 / math.sqrt(head_size)
    query_heads = queries.reshape(row_count, head_count, head_size).astype(jnp.float32)
    upstream_heads = upstream.reshape(row_count, head_count, head_size).astype(jnp.float32)
    key_heads = key_rows.reshape(key_count, head_count, head_size).astype(jnp.float32)
    value_heads = value_rows.reshape(key_count, head_count, head_size).astype(jnp.float32)
    raw_score = jnp.einsum('qhd,khd->hqk', query_heads, key_heads) * inv_root
    logits = jnp.where(allowed[None, :, :], gain_logit[:, None, None] * raw_score, masked_score)
    row_top = lax.optimization_barrier(jnp.max(logits, axis=2, keepdims=True))
    lifted = jnp.exp(logits - row_top)
    chances = lifted / lax.optimization_barrier(jnp.sum(lifted, axis=2, keepdims=True))
    chances_low = chances.astype(jnp.bfloat16).astype(jnp.float32)
    attended = (jnp.einsum('hqk,khd->qhd', chances_low, value_heads) * gain_value[None, :, None]).astype(jnp.bfloat16)
    slope = jnp.einsum('qhd,khd->hqk', upstream_heads, value_heads) * gain_value[:, None, None]
    carried = jnp.einsum('qhd,qhd->hq', upstream_heads, attended.astype(jnp.float32))
    score_grad = chances * (slope - carried[:, :, None])
    score_low = score_grad.astype(jnp.bfloat16).astype(jnp.float32)
    factor = gain_logit * inv_root
    query_grad = jnp.einsum('hqk,khd->qhd', score_low, key_heads) * factor[None, :, None]
    key_grad = jnp.einsum('hqk,qhd->khd', score_low, query_heads) * factor[None, :, None]
    value_grad = jnp.einsum('hqk,qhd->khd', chances_low, upstream_heads) * gain_value[None, :, None]
    gain_term = lax.optimization_barrier(jnp.sum(score_grad * raw_score, axis=(1, 2)))
    return (attended.reshape(row_count, -1), query_grad.reshape(row_count, -1), key_grad.reshape(key_count, -1), value_grad.reshape(key_count, -1), gain_term)

def reference(sections, head_gains, block_counts):
    block_total = BLK_DEV * N_SEQ
    span_blocks = BLK_DEV + 6
    group_rows = block_total * BLOCK
    key_all = sections[0, 0]
    value_all = sections[0, 1]
    query_all = sections[1, 0]
    upstream_all = sections[1, 1]
    gain_logit = head_gains[0]
    gain_value = head_gains[1]

    def one_device(grad_sum, device_index):
        group_index = (device_index // N_SEQ).astype(jnp.int32)
        shard_index = (device_index % N_SEQ).astype(jnp.int32)
        group_counts = lax.dynamic_index_in_dim(block_counts, group_index, 0, keepdims=False)
        enc_counts = group_counts[0]
        dec_counts = group_counts[1]
        enc_starts = (jnp.cumsum(enc_counts) - enc_counts).astype(jnp.int32)
        span_low = jnp.clip(shard_index * BLK_DEV - 2, 0, block_total - span_blocks).astype(jnp.int32)
        group_base = (group_index * group_rows).astype(jnp.int32)
        partial_value = jnp.zeros((2, span_blocks * BLOCK, INNER), jnp.float32)
        row_parts = []
        gain_total = jnp.zeros((H,), jnp.float32)
        for offset in range(BLK_DEV):
            block_index = (shard_index * BLK_DEV + offset).astype(jnp.int32)
            segment = segment_of(jnp.reshape(block_index, (1,)), dec_counts, block_total)[0]
            slice_first = jnp.clip(enc_starts[segment], 0, block_total - ENC_MOST).astype(jnp.int32)
            slice_segs = segment_of(slice_first + jnp.arange(ENC_MOST, dtype=jnp.int32), enc_counts, block_total)
            allowed = jnp.broadcast_to(jnp.repeat(slice_segs == segment, BLOCK)[None, :], (BLOCK, ENC_MOST * BLOCK))
            query_start = (group_base + block_index * BLOCK).astype(jnp.int32)
            key_start = (group_base + slice_first * BLOCK).astype(jnp.int32)
            queries = lax.dynamic_slice_in_dim(query_all, query_start, BLOCK, 0)
            upstream = lax.dynamic_slice_in_dim(upstream_all, query_start, BLOCK, 0)
            key_rows = lax.dynamic_slice_in_dim(key_all, key_start, ENC_MOST * BLOCK, 0)
            value_rows = lax.dynamic_slice_in_dim(value_all, key_start, ENC_MOST * BLOCK, 0)
            attended, query_grad, key_grad, value_grad, gain_term = cross_tile(queries, upstream, key_rows, value_rows, allowed, gain_logit, gain_value)
            write_at = ((slice_first - span_low) * BLOCK).astype(jnp.int32)
            current = lax.dynamic_slice_in_dim(partial_value, write_at, ENC_MOST * BLOCK, 1)
            partial_value = lax.dynamic_update_slice_in_dim(partial_value, current + jnp.stack([key_grad, value_grad]), write_at, 1)
            row_parts.append(jnp.stack([attended, query_grad.astype(jnp.bfloat16)]))
            gain_total = gain_total + gain_term
        rounded = lax.optimization_barrier(partial_value.astype(jnp.bfloat16)).astype(jnp.float32)
        position = (group_base + span_low * BLOCK).astype(jnp.int32)
        current = lax.dynamic_slice_in_dim(grad_sum, position, span_blocks * BLOCK, 1)
        grad_sum = lax.dynamic_update_slice_in_dim(grad_sum, current + rounded, position, 1)
        return (grad_sum, (jnp.concatenate(row_parts, axis=1), gain_total))
    start_sum = jnp.zeros((2, TOKENS, INNER), jnp.float32)
    grad_sum, (row_blocks, gain_terms) = lax.scan(one_device, start_sum, jnp.arange(N_DP * N_SEQ, dtype=jnp.int32))
    decoder_rows = jnp.transpose(row_blocks, (1, 0, 2, 3)).reshape(2, TOKENS, INNER)
    encoder_rows = grad_sum.astype(jnp.bfloat16)
    root_tokens = math.sqrt(TOKENS)
    logit_grad = lax.optimization_barrier(jnp.sum(gain_terms, axis=0)) / root_tokens
    value_heads = value_all.reshape(TOKENS, H, HD).astype(jnp.float32)
    value_grad_heads = encoder_rows[1].reshape(TOKENS, H, HD).astype(jnp.float32)
    value_gain_grad = jnp.einsum('thd,thd->h', value_heads, value_grad_heads) / (gain_value * root_tokens)
    result = jnp.stack([encoder_rows, decoder_rows])
    gain_grads = jnp.stack([value_gain_grad, logit_grad])
    return (result, gain_grads)
```

```python
import math

import jax
import jax.numpy as jnp
from jax import lax
from jax.sharding import PartitionSpec as P

BLOCK = 128
ENC_MOST = 4
BLK_DEV = 1
REACH_LOW = 2
REACH_HIGH = 3
WINDOW = 6


masked_score = -1e30
heads_per_pass = 4


def passed_along(value, axis, steps):
    count = lax.axis_size(axis)
    initial, last = (max(0, -steps), min(count, count - steps))
    return lax.ppermute(value, axis, [(source, source + steps) for source in range(initial, last)])


def decoder_along(value, steps):
    count = lax.axis_size("seq")
    initial, last = (max(0, -steps), min(count, count - steps))
    pairs = [(count + source, count + source + steps) for source in range(initial, last)]
    return lax.ppermute(value, ("phase", "seq"), pairs)


def segment_of(block_ids, block_sizes, block_total):
    starts = jnp.cumsum(block_sizes) - block_sizes
    found = jnp.sum((starts[None, :] <= block_ids[:, None]).astype(jnp.int32), axis=1) - 1
    inside = jnp.logical_and(block_ids >= 0, block_ids < block_total)
    return jnp.where(inside, found, -1)


def cross_tile(queries, upstream, key_rows, value_rows, allowed, gain_logit, gain_value):
    row_count = queries.shape[0]
    key_count = key_rows.shape[0]
    head_count = gain_logit.shape[0]
    head_size = queries.shape[1] // head_count
    inv_root = 1.0 / math.sqrt(head_size)
    query_heads = queries.reshape(row_count, head_count, head_size)
    upstream_heads = upstream.reshape(row_count, head_count, head_size)
    key_heads = key_rows.reshape(key_count, head_count, head_size)
    value_heads = value_rows.reshape(key_count, head_count, head_size)
    raw_score = (
        jnp.einsum("qhd,khd->hqk", query_heads, key_heads, preferred_element_type=jnp.float32)
        * inv_root
    )
    logits = jnp.where(allowed[None, :, :], gain_logit[:, None, None] * raw_score, masked_score)
    row_top = jnp.max(logits, axis=2, keepdims=True)
    lifted = jnp.exp(logits - row_top)
    chances = lifted / jnp.sum(lifted, axis=2, keepdims=True)
    chances_low = chances.astype(jnp.bfloat16)
    attended = (
        jnp.einsum("hqk,khd->qhd", chances_low, value_heads, preferred_element_type=jnp.float32)
        * gain_value[None, :, None]
    ).astype(jnp.bfloat16)
    slope = (
        jnp.einsum("qhd,khd->hqk", upstream_heads, value_heads, preferred_element_type=jnp.float32)
        * gain_value[:, None, None]
    )
    carried = jnp.einsum(
        "qhd,qhd->hq", upstream_heads, attended, preferred_element_type=jnp.float32
    )
    score_grad = chances * (slope - carried[:, :, None])
    score_low = score_grad.astype(jnp.bfloat16)
    factor = gain_logit * inv_root
    query_grad = (
        jnp.einsum("hqk,khd->qhd", score_low, key_heads, preferred_element_type=jnp.float32)
        * factor[None, :, None]
    )
    key_grad = (
        jnp.einsum("hqk,qhd->khd", score_low, query_heads, preferred_element_type=jnp.float32)
        * factor[None, :, None]
    )
    value_grad = (
        jnp.einsum("hqk,qhd->khd", chances_low, upstream_heads, preferred_element_type=jnp.float32)
        * gain_value[None, :, None]
    )
    gain_term = jnp.sum(score_grad * raw_score, axis=(1, 2))
    return (
        attended.reshape(row_count, -1),
        query_grad.reshape(row_count, -1),
        key_grad.reshape(key_count, -1),
        value_grad.reshape(key_count, -1),
        gain_term,
    )


def head_passes(queries, upstream, key_rows, value_rows, allowed, head_gains):
    head_count = head_gains.shape[1]
    head_size = queries.shape[1] // head_count
    results = []
    for first_head in range(0, head_count, heads_per_pass):
        low_col = first_head * head_size
        high_col = low_col + heads_per_pass * head_size
        results.append(
            cross_tile(
                queries[:, low_col:high_col],
                upstream[:, low_col:high_col],
                key_rows[:, low_col:high_col],
                value_rows[:, low_col:high_col],
                allowed,
                head_gains[0, first_head : first_head + heads_per_pass],
                head_gains[1, first_head : first_head + heads_per_pass],
            )
        )
    return tuple(
        (jnp.concatenate([piece[member] for piece in results], axis=-1) for member in range(5))
    )


def local(sections, head_gains, block_counts):
    phase_index = lax.axis_index("phase")
    shard_index = lax.axis_index("seq")
    local_pair = sections[0]
    tok_dev = local_pair.shape[1]
    inner_width = local_pair.shape[2]
    head_count = head_gains.shape[1]
    block_total = BLK_DEV * lax.axis_size("seq")
    enc_counts = block_counts[0, 0]
    dec_counts = block_counts[0, 1]
    offsets = list(range(-REACH_LOW, REACH_HIGH + 1))
    arrived = passed_along(local_pair, "phase", 1)
    pieces = []
    for offset in offsets:
        if offset == 0:
            pieces.append(arrived)
        else:
            pieces.append(decoder_along(arrived, -offset))
    window = jnp.concatenate(pieces, axis=1)
    window_rows = window.shape[1]

    def decoder_work(operands):
        own_pair, window_pair = operands
        first_block = (shard_index - REACH_LOW) * BLK_DEV
        window_blocks = first_block + jnp.arange(WINDOW * BLK_DEV, dtype=jnp.int32)
        enc_segs = segment_of(window_blocks, enc_counts, block_total)
        dec_blocks = shard_index * BLK_DEV + jnp.arange(BLK_DEV, dtype=jnp.int32)
        dec_segs = segment_of(dec_blocks, dec_counts, block_total)
        enc_starts = jnp.cumsum(enc_counts) - enc_counts
        key_sum = jnp.zeros((window_rows, inner_width), jnp.float32)
        value_sum = jnp.zeros((window_rows, inner_width), jnp.float32)
        gain_term = jnp.zeros((head_count,), jnp.float32)
        segment = dec_segs[0]
        start_block = jnp.clip(enc_starts[segment] - first_block, 0, WINDOW * BLK_DEV - ENC_MOST)
        slice_segs = lax.dynamic_slice_in_dim(enc_segs, start_block, ENC_MOST)
        allowed = jnp.broadcast_to(
            jnp.repeat(slice_segs == segment, BLOCK)[None, :], (BLOCK, ENC_MOST * BLOCK)
        )
        key_slice = lax.dynamic_slice_in_dim(
            window_pair[0], start_block * BLOCK, ENC_MOST * BLOCK, 0
        )
        value_slice = lax.dynamic_slice_in_dim(
            window_pair[1], start_block * BLOCK, ENC_MOST * BLOCK, 0
        )
        attended, query_grad, key_grad, value_grad, block_gain = head_passes(
            own_pair[0, 0:BLOCK], own_pair[1, 0:BLOCK], key_slice, value_slice, allowed, head_gains
        )
        write_at = start_block * BLOCK
        key_sum = lax.dynamic_update_slice_in_dim(
            key_sum,
            lax.dynamic_slice_in_dim(key_sum, write_at, ENC_MOST * BLOCK, 0) + key_grad,
            write_at,
            0,
        )
        value_sum = lax.dynamic_update_slice_in_dim(
            value_sum,
            lax.dynamic_slice_in_dim(value_sum, write_at, ENC_MOST * BLOCK, 0) + value_grad,
            write_at,
            0,
        )
        attended_rows = [attended]
        query_rows = [query_grad.astype(jnp.bfloat16)]
        gain_term = gain_term + block_gain
        produced = jnp.stack(
            [jnp.concatenate(attended_rows, axis=0), jnp.concatenate(query_rows, axis=0)]
        )
        window_grads = jnp.stack([key_sum.astype(jnp.bfloat16), value_sum.astype(jnp.bfloat16)])
        return (produced, window_grads, gain_term)

    def encoder_rest(operands):
        return (
            jnp.zeros((2, tok_dev, inner_width), jnp.bfloat16),
            jnp.zeros((2, window_rows, inner_width), jnp.bfloat16),
            jnp.zeros((head_count,), jnp.float32),
        )

    produced, window_grads, gain_term = lax.cond(
        phase_index == 1, decoder_work, encoder_rest, (local_pair, window)
    )
    summed_grads = jnp.zeros((2, tok_dev, inner_width), jnp.float32)
    for slot, offset in enumerate(offsets):
        portion = window_grads[:, slot * tok_dev : (slot + 1) * tok_dev]
        if offset == 0:
            summed_grads = summed_grads + portion.astype(jnp.float32)
        else:
            summed_grads = summed_grads + decoder_along(portion, offset).astype(jnp.float32)
    returned = passed_along(summed_grads.astype(jnp.bfloat16), "phase", -1)
    value_heads = local_pair[1].reshape(tok_dev, head_count, -1)
    value_grad_heads = returned[1].reshape(tok_dev, head_count, -1)
    value_term = (
        jnp.einsum("thd,thd->h", value_heads, value_grad_heads, preferred_element_type=jnp.float32)
        / head_gains[1]
    )
    chosen_term = jnp.where(phase_index == 0, value_term, gain_term)
    token_total = tok_dev * lax.axis_size("seq") * lax.axis_size("dp")
    slots = jnp.where(
        jnp.arange(2, dtype=jnp.int32)[:, None] == phase_index, chosen_term[None, :], 0.0
    )
    summed = lax.psum(slots, ("phase", "seq", "dp"))
    gain_total = lax.dynamic_index_in_dim(summed, phase_index, 0, keepdims=False) / math.sqrt(token_total)
    result = jnp.where(phase_index == 0, returned, produced)[None]
    return (result, gain_total[None])


def solution(mesh):
    return jax.shard_map(
        local,
        mesh=mesh,
        in_specs=(P("phase", None, ("dp", "seq"), None), P(), P("dp", None, None)),
        out_specs=(P("phase", None, ("dp", "seq"), None), P("phase", None)),
        check_vma=False,
    )
```

```python
import math

import jax
import jax.numpy as jnp
from jax import lax
from jax.experimental import pallas as pl
from jax.experimental.pallas import tpu as pltpu
from jax.sharding import PartitionSpec as P

BLOCK = 128
ENC_MOST = 4
BLK_DEV = 1
REACH_LOW = 2
REACH_HIGH = 3
WINDOW = 6


masked_score = -1e30
heads_per_pass = 4


def attention_kernel(gains_ref, q_ref, do_ref, k_ref, v_ref, allow_ref,
                     att_ref, dq_ref, dk_ref, dv_ref, gain_ref):
    pair = pl.program_id(0)
    width = q_ref.shape[1]
    half = width // 2
    inv_root = 1.0 / math.sqrt(half)
    q = q_ref[...]
    do = do_ref[...]
    k = k_ref[...]
    v = v_ref[...]
    allowed = allow_ref[...] > 0
    lane = lax.broadcasted_iota(jnp.int32, (1, width), 1)
    first = lane < half
    zero_q = jnp.zeros_like(q)
    att_f = []
    p_lows = []
    raws = []
    chances_all = []
    for j in range(2):
        head = pair * 2 + j
        g_logit = gains_ref[0, head]
        g_value = gains_ref[1, head]
        mine = first if j == 0 else jnp.logical_not(first)
        q_h = jnp.where(mine, q, zero_q)
        raw = lax.dot_general(q_h, k, (((1,), (1,)), ((), ())), preferred_element_type=jnp.float32) * inv_root
        logits = jnp.where(allowed, g_logit * raw, masked_score)
        top = jnp.max(logits, axis=1, keepdims=True)
        lifted = jnp.exp(logits - top)
        chances = lifted / jnp.sum(lifted, axis=1, keepdims=True)
        p_low = chances.astype(jnp.bfloat16)
        att_full = jnp.dot(p_low, v, preferred_element_type=jnp.float32) * g_value
        att_f.append(att_full)
        p_lows.append(p_low)
        raws.append(raw)
        chances_all.append(chances)
    attended = jnp.where(first, att_f[0], att_f[1]).astype(jnp.bfloat16)
    att_ref[...] = attended
    prod = do.astype(jnp.float32) * attended.astype(jnp.float32)
    dq_parts, dk_parts, dv_parts, gain_vals = [], [], [], []
    zero_do = jnp.zeros_like(do)
    for j in range(2):
        head = pair * 2 + j
        g_logit = gains_ref[0, head]
        g_value = gains_ref[1, head]
        mine = first if j == 0 else jnp.logical_not(first)
        do_h = jnp.where(mine, do, zero_do)
        slope = lax.dot_general(do_h, v, (((1,), (1,)), ((), ())), preferred_element_type=jnp.float32) * g_value
        carried = jnp.sum(jnp.where(mine, prod, 0.0), axis=1, keepdims=True)
        score_grad = chances_all[j] * (slope - carried)
        score_low = score_grad.astype(jnp.bfloat16)
        factor = g_logit * inv_root
        dq_parts.append(jnp.dot(score_low, k, preferred_element_type=jnp.float32) * factor)
        dk_parts.append(lax.dot_general(score_low, q, (((0,), (0,)), ((), ())), preferred_element_type=jnp.float32) * factor)
        dv_parts.append(lax.dot_general(p_lows[j], do, (((0,), (0,)), ((), ())), preferred_element_type=jnp.float32) * g_value)
        gain_vals.append(jnp.sum(score_grad * raws[j]))
    dq_ref[...] = jnp.where(first, dq_parts[0], dq_parts[1]).astype(dq_ref.dtype)
    dk_ref[...] = jnp.where(first, dk_parts[0], dk_parts[1]).astype(dk_ref.dtype)
    dv_ref[...] = jnp.where(first, dv_parts[0], dv_parts[1]).astype(dv_ref.dtype)
    glane = lax.broadcasted_iota(jnp.int32, gain_ref.shape, 2)
    gain_ref[...] = jnp.where(glane == 0, gain_vals[0], jnp.where(glane == 1, gain_vals[1], 0.0))


def attention_block(q, do, k, v, allowed_keys, head_gains):
    rows, inner = q.shape
    keys = k.shape[0]
    head_count = head_gains.shape[1]
    width = 2 * (inner // head_count)
    pairs = inner // width
    row_spec = pl.BlockSpec((rows, width), lambda i, g: (0, i))
    key_spec = pl.BlockSpec((keys, width), lambda i, g: (0, i))
    grid_spec = pltpu.PrefetchScalarGridSpec(
        num_scalar_prefetch=1,
        grid=(pairs,),
        in_specs=[row_spec, row_spec, key_spec, key_spec, pl.BlockSpec((1, keys), lambda i, g: (0, 0))],
        out_specs=[row_spec, row_spec, key_spec, key_spec, pl.BlockSpec((1, 8, 128), lambda i, g: (i, 0, 0))],
    )
    flops = 2 * rows * keys * width * 6 * pairs * 2
    cost = pl.CostEstimate(flops=flops, transcendentals=rows * keys * head_count,
                           bytes_accessed=2 * (4 * rows * inner + 4 * keys * inner))
    att, dq, dk, dv, gains = pl.pallas_call(
        attention_kernel,
        grid_spec=grid_spec,
        out_shape=[
            jax.ShapeDtypeStruct((rows, inner), jnp.bfloat16),
            jax.ShapeDtypeStruct((rows, inner), jnp.bfloat16),
            jax.ShapeDtypeStruct((keys, inner), jnp.bfloat16),
            jax.ShapeDtypeStruct((keys, inner), jnp.bfloat16),
            jax.ShapeDtypeStruct((pairs, 8, 128), jnp.float32),
        ],
        cost_estimate=cost,
    )(head_gains, q, do, k, v, allowed_keys.astype(jnp.int32)[None, :])
    gain_term = gains[:, 0, :2].reshape(-1)
    return att, dq, dk, dv, gain_term


def passed_along(value, axis, steps):
    count = lax.axis_size(axis)
    initial, last = (max(0, -steps), min(count, count - steps))
    return lax.ppermute(value, axis, [(source, source + steps) for source in range(initial, last)])


def butterfly_sum(value, axis):
    count = lax.axis_size(axis)
    stride = 1
    while stride < count:
        value = value + lax.ppermute(value, axis, [(i, i ^ stride) for i in range(count)])
        stride *= 2
    return value


def decoder_along(value, steps):
    count = lax.axis_size("seq")
    initial, last = (max(0, -steps), min(count, count - steps))
    pairs = [(count + source, count + source + steps) for source in range(initial, last)]
    return lax.ppermute(value, ("phase", "seq"), pairs)


def segment_of(block_ids, block_sizes, block_total):
    starts = jnp.cumsum(block_sizes) - block_sizes
    found = jnp.sum((starts[None, :] <= block_ids[:, None]).astype(jnp.int32), axis=1) - 1
    inside = jnp.logical_and(block_ids >= 0, block_ids < block_total)
    return jnp.where(inside, found, -1)


def cross_tile(queries, upstream, key_rows, value_rows, allowed, gain_logit, gain_value):
    row_count = queries.shape[0]
    key_count = key_rows.shape[0]
    head_count = gain_logit.shape[0]
    head_size = queries.shape[1] // head_count
    inv_root = 1.0 / math.sqrt(head_size)
    query_heads = queries.reshape(row_count, head_count, head_size)
    upstream_heads = upstream.reshape(row_count, head_count, head_size)
    key_heads = key_rows.reshape(key_count, head_count, head_size)
    value_heads = value_rows.reshape(key_count, head_count, head_size)
    raw_score = (
        jnp.einsum("qhd,khd->hqk", query_heads, key_heads, preferred_element_type=jnp.float32)
        * inv_root
    )
    logits = jnp.where(allowed[None, :, :], gain_logit[:, None, None] * raw_score, masked_score)
    row_top = jnp.max(logits, axis=2, keepdims=True)
    lifted = jnp.exp(logits - row_top)
    chances = lifted / jnp.sum(lifted, axis=2, keepdims=True)
    chances_low = chances.astype(jnp.bfloat16)
    attended = (
        jnp.einsum("hqk,khd->qhd", chances_low, value_heads, preferred_element_type=jnp.float32)
        * gain_value[None, :, None]
    ).astype(jnp.bfloat16)
    slope = (
        jnp.einsum("qhd,khd->hqk", upstream_heads, value_heads, preferred_element_type=jnp.float32)
        * gain_value[:, None, None]
    )
    carried = jnp.einsum(
        "qhd,qhd->hq", upstream_heads, attended, preferred_element_type=jnp.float32
    )
    score_grad = chances * (slope - carried[:, :, None])
    score_low = score_grad.astype(jnp.bfloat16)
    factor = gain_logit * inv_root
    query_grad = (
        jnp.einsum("hqk,khd->qhd", score_low, key_heads, preferred_element_type=jnp.float32)
        * factor[None, :, None]
    )
    key_grad = (
        jnp.einsum("hqk,qhd->khd", score_low, query_heads, preferred_element_type=jnp.float32)
        * factor[None, :, None]
    )
    value_grad = (
        jnp.einsum("hqk,qhd->khd", chances_low, upstream_heads, preferred_element_type=jnp.float32)
        * gain_value[None, :, None]
    )
    gain_term = jnp.sum(score_grad * raw_score, axis=(1, 2))
    return (
        attended.reshape(row_count, -1),
        query_grad.reshape(row_count, -1),
        key_grad.reshape(key_count, -1),
        value_grad.reshape(key_count, -1),
        gain_term,
    )


def head_passes(queries, upstream, key_rows, value_rows, allowed, head_gains):
    head_count = head_gains.shape[1]
    head_size = queries.shape[1] // head_count
    results = []
    for first_head in range(0, head_count, heads_per_pass):
        low_col = first_head * head_size
        high_col = low_col + heads_per_pass * head_size
        results.append(
            cross_tile(
                queries[:, low_col:high_col],
                upstream[:, low_col:high_col],
                key_rows[:, low_col:high_col],
                value_rows[:, low_col:high_col],
                allowed,
                head_gains[0, first_head : first_head + heads_per_pass],
                head_gains[1, first_head : first_head + heads_per_pass],
            )
        )
    return tuple(
        (jnp.concatenate([piece[member] for piece in results], axis=-1) for member in range(5))
    )


def local(sections, head_gains, block_counts):
    phase_index = lax.axis_index("phase")
    shard_index = lax.axis_index("seq")
    local_pair = sections[0]
    tok_dev = local_pair.shape[1]
    inner_width = local_pair.shape[2]
    head_count = head_gains.shape[1]
    block_total = BLK_DEV * lax.axis_size("seq")
    enc_counts = block_counts[0, 0]
    dec_counts = block_counts[0, 1]
    offsets = list(range(-REACH_LOW, REACH_HIGH + 1))
    arrived = passed_along(local_pair, "phase", 1)
    pieces = []
    for offset in offsets:
        if offset == 0:
            pieces.append(arrived)
        else:
            pieces.append(decoder_along(arrived, -offset))
    window = jnp.concatenate(pieces, axis=1)
    window_rows = window.shape[1]

    def decoder_work(operands):
        own_pair, window_pair = operands
        first_block = (shard_index - REACH_LOW) * BLK_DEV
        window_blocks = first_block + jnp.arange(WINDOW * BLK_DEV, dtype=jnp.int32)
        enc_segs = segment_of(window_blocks, enc_counts, block_total)
        dec_blocks = shard_index * BLK_DEV + jnp.arange(BLK_DEV, dtype=jnp.int32)
        dec_segs = segment_of(dec_blocks, dec_counts, block_total)
        enc_starts = jnp.cumsum(enc_counts) - enc_counts
        segment = dec_segs[0]
        start_block = jnp.clip(enc_starts[segment] - first_block, 0, WINDOW * BLK_DEV - ENC_MOST)
        slice_segs = lax.dynamic_slice_in_dim(enc_segs, start_block, ENC_MOST)
        allowed_keys = jnp.repeat(slice_segs == segment, BLOCK)
        key_slice = lax.dynamic_slice_in_dim(
            window_pair[0], start_block * BLOCK, ENC_MOST * BLOCK, 0
        )
        value_slice = lax.dynamic_slice_in_dim(
            window_pair[1], start_block * BLOCK, ENC_MOST * BLOCK, 0
        )
        attended, query_grad, key_grad, value_grad, gain_term = attention_block(
            own_pair[0, 0:BLOCK], own_pair[1, 0:BLOCK], key_slice, value_slice, allowed_keys, head_gains
        )
        write_at = start_block * BLOCK
        grads = jnp.stack([key_grad, value_grad])
        window_grads = lax.dynamic_update_slice_in_dim(
            jnp.zeros((2, window_rows, inner_width), jnp.bfloat16), grads, write_at, 1
        )
        produced = jnp.stack([attended, query_grad])
        return (produced, window_grads, gain_term)

    def encoder_rest(operands):
        return (
            jnp.zeros((2, tok_dev, inner_width), jnp.bfloat16),
            jnp.zeros((2, window_rows, inner_width), jnp.bfloat16),
            jnp.zeros((head_count,), jnp.float32),
        )

    produced, window_grads, gain_term = lax.cond(
        phase_index == 1, decoder_work, encoder_rest, (local_pair, window)
    )
    summed_grads = jnp.zeros((2, tok_dev, inner_width), jnp.float32)
    for slot, offset in enumerate(offsets):
        portion = window_grads[:, slot * tok_dev : (slot + 1) * tok_dev]
        if offset == 0:
            summed_grads = summed_grads + portion.astype(jnp.float32)
        else:
            summed_grads = summed_grads + decoder_along(portion, offset).astype(jnp.float32)
    returned = passed_along(summed_grads.astype(jnp.bfloat16), "phase", -1)
    value_heads = local_pair[1].reshape(tok_dev, head_count, -1)
    value_grad_heads = returned[1].reshape(tok_dev, head_count, -1)
    value_term = (
        jnp.einsum("thd,thd->h", value_heads, value_grad_heads, preferred_element_type=jnp.float32)
        / head_gains[1]
    )
    chosen_term = jnp.where(phase_index == 0, value_term, gain_term)
    token_total = tok_dev * lax.axis_size("seq") * lax.axis_size("dp")
    summed = butterfly_sum(butterfly_sum(chosen_term, "dp"), "seq")
    gain_total = summed / math.sqrt(token_total)
    result = jnp.where(phase_index == 0, returned, produced)[None]
    return (result, gain_total[None])


def solution(mesh):
    return jax.shard_map(
        local,
        mesh=mesh,
        in_specs=(P("phase", None, ("dp", "seq"), None), P(), P("dp", None, None)),
        out_specs=(P("phase", None, ("dp", "seq"), None), P("phase", None)),
        check_vma=False,
    )
```

```python
import math

import jax
import jax.numpy as jnp
from jax import lax
from jax.experimental import pallas as pl
from jax.experimental.pallas import tpu as pltpu
from jax.sharding import PartitionSpec as P

BLOCK = 128
ENC_MOST = 4
REACH_LOW = 2
REACH_HIGH = 3
WINDOW = REACH_LOW + REACH_HIGH + 1

masked_score = -1e30


def attention_kernel(start_ref, gains_ref, own_ref, *refs):
    window_refs = refs[:WINDOW]
    allow_ref = refs[WINDOW]
    out_ref = refs[WINDOW + 1]
    grad_refs = refs[WINDOW + 2 : 2 * WINDOW + 2]
    gain_ref = refs[2 * WINDOW + 2]
    pair = pl.program_id(0)
    start = start_ref[0]
    width = own_ref.shape[2]
    half = width // 2
    inv_root = 1.0 / math.sqrt(half)
    q = own_ref[0]
    do = own_ref[1]
    blocks = [ref[...] for ref in window_refs]

    def pick(slot):
        chosen = blocks[slot + WINDOW - ENC_MOST]
        for shift in range(WINDOW - ENC_MOST - 1, -1, -1):
            chosen = jnp.where(start == shift, blocks[slot + shift], chosen)
        return chosen

    slots = [pick(slot) for slot in range(ENC_MOST)]
    k = jnp.concatenate([piece[0] for piece in slots], axis=0)
    v = jnp.concatenate([piece[1] for piece in slots], axis=0)
    allowed = allow_ref[...] > 0
    lane = lax.broadcasted_iota(jnp.int32, (1, width), 1)
    first = lane < half
    heads = []
    att_parts = []
    for j in range(2):
        head = pair * 2 + j
        g_logit = gains_ref[0, head]
        g_value = gains_ref[1, head]
        mine = first if j == 0 else jnp.logical_not(first)
        q_h = jnp.where(mine, q, jnp.zeros_like(q))
        raw = lax.dot_general(q_h, k, (((1,), (1,)), ((), ())), preferred_element_type=jnp.float32) * inv_root
        logits = jnp.where(allowed, g_logit * raw, masked_score)
        top = jnp.max(logits, axis=1, keepdims=True)
        lifted = jnp.exp(logits - top)
        chances = lifted / jnp.sum(lifted, axis=1, keepdims=True)
        p_low = chances.astype(jnp.bfloat16)
        att_parts.append(jnp.dot(p_low, v, preferred_element_type=jnp.float32) * g_value)
        heads.append((g_logit, g_value, mine, raw, chances, p_low))
    attended = jnp.where(first, att_parts[0], att_parts[1]).astype(jnp.bfloat16)
    out_ref[0] = attended
    prod = do.astype(jnp.float32) * attended.astype(jnp.float32)
    dq_parts, dk_parts, dv_parts, logit_terms = [], [], [], []
    for g_logit, g_value, mine, raw, chances, p_low in heads:
        do_h = jnp.where(mine, do, jnp.zeros_like(do))
        slope = lax.dot_general(do_h, v, (((1,), (1,)), ((), ())), preferred_element_type=jnp.float32) * g_value
        carried = jnp.sum(jnp.where(mine, prod, 0.0), axis=1, keepdims=True)
        score_grad = chances * (slope - carried)
        score_low = score_grad.astype(jnp.bfloat16)
        factor = g_logit * inv_root
        dq_parts.append(jnp.dot(score_low, k, preferred_element_type=jnp.float32) * factor)
        dk_parts.append(lax.dot_general(score_low, q, (((0,), (0,)), ((), ())), preferred_element_type=jnp.float32) * factor)
        dv_parts.append(lax.dot_general(p_low, do, (((0,), (0,)), ((), ())), preferred_element_type=jnp.float32) * g_value)
        logit_terms.append(jnp.sum(score_grad * raw))
    out_ref[1] = jnp.where(first, dq_parts[0], dq_parts[1]).astype(jnp.bfloat16)
    key_grad = jnp.where(first, dk_parts[0], dk_parts[1]).astype(jnp.bfloat16)
    value_grad = jnp.where(first, dv_parts[0], dv_parts[1]).astype(jnp.bfloat16)
    value_prod = v.astype(jnp.float32) * value_grad.astype(jnp.float32)
    value_terms = [jnp.sum(jnp.where(first, value_prod, 0.0)), jnp.sum(jnp.where(first, 0.0, value_prod))]
    zero_block = jnp.zeros((BLOCK, width), jnp.bfloat16)
    for position in range(WINDOW):
        key_block = zero_block
        value_block = zero_block
        for slot in range(ENC_MOST):
            if 0 <= position - slot <= WINDOW - ENC_MOST:
                rows = slice(slot * BLOCK, (slot + 1) * BLOCK)
                key_block = jnp.where(start == position - slot, key_grad[rows], key_block)
                value_block = jnp.where(start == position - slot, value_grad[rows], value_block)
        grad_refs[position][0] = key_block
        grad_refs[position][1] = value_block
    glane = lax.broadcasted_iota(jnp.int32, gain_ref.shape, 2)
    terms = value_terms + logit_terms
    packed = jnp.zeros(gain_ref.shape, jnp.float32)
    for index, term in enumerate(terms):
        packed = jnp.where(glane == index, term, packed)
    gain_ref[...] = packed


def attention_block(start, head_gains, own, window, allowed_keys):
    _, rows, inner = own.shape
    keys = ENC_MOST * BLOCK
    head_count = head_gains.shape[1]
    width = 2 * (inner // head_count)
    pairs = inner // width
    block_spec = pl.BlockSpec((2, rows, width), lambda i, s, g: (0, 0, i))
    grid_spec = pltpu.PrefetchScalarGridSpec(
        num_scalar_prefetch=2,
        grid=(pairs,),
        in_specs=[block_spec] * (WINDOW + 1) + [pl.BlockSpec((1, keys), lambda i, s, g: (0, 0))],
        out_specs=[block_spec] * (WINDOW + 1) + [pl.BlockSpec((1, 8, 128), lambda i, s, g: (i, 0, 0))],
    )
    flops = 2 * rows * keys * width * 6 * pairs * 2
    cost = pl.CostEstimate(
        flops=flops,
        transcendentals=rows * keys * head_count,
        bytes_accessed=2 * 2 * rows * inner * (2 * WINDOW + 2),
    )
    outs = pl.pallas_call(
        attention_kernel,
        grid_spec=grid_spec,
        out_shape=[jax.ShapeDtypeStruct(own.shape, jnp.bfloat16)] * (WINDOW + 1)
        + [jax.ShapeDtypeStruct((pairs, 8, 128), jnp.float32)],
        cost_estimate=cost,
    )(start, head_gains, own, *window, allowed_keys.astype(jnp.int32)[None, :])
    produced = outs[0]
    grads = tuple(outs[1 : WINDOW + 1])
    packed = outs[WINDOW + 1]
    terms = jnp.stack([packed[:, 0, 0:2].reshape(-1), packed[:, 0, 2:4].reshape(-1)])
    return produced, grads, terms


def butterfly_sum(value, axis):
    count = lax.axis_size(axis)
    stride = 1
    while stride < count:
        value = value + lax.ppermute(value, axis, [(i, i ^ stride) for i in range(count)])
        stride *= 2
    return value


def segment_of(block_ids, block_sizes, block_total):
    starts = jnp.cumsum(block_sizes) - block_sizes
    found = jnp.sum((starts[None, :] <= block_ids[:, None]).astype(jnp.int32), axis=1) - 1
    inside = jnp.logical_and(block_ids >= 0, block_ids < block_total)
    return jnp.where(inside, found, -1)


def local(sections, head_gains, block_counts):
    phase_index = lax.axis_index("phase")
    shard_index = lax.axis_index("seq")
    count = lax.axis_size("seq")
    local_pair = sections[0]
    tok_dev = local_pair.shape[1]
    head_count = head_gains.shape[1]
    enc_counts = block_counts[0, 0]
    dec_counts = block_counts[0, 1]

    def enc(s):
        return s

    def dec(s):
        return count + s

    def across(value, pairs):
        return lax.ppermute(value, ("phase", "seq"), pairs)

    lower = range(count - 1)
    upper = range(1, count)
    at_home = across(local_pair, [(enc(s), dec(s)) for s in range(count)])
    minus_1 = across(local_pair, [(enc(s + 1), dec(s)) for s in lower])
    plus_1 = across(local_pair, [(enc(s - 1), dec(s)) for s in upper])
    minus_2 = across(minus_1, [(dec(s + 1), dec(s)) for s in lower])
    plus_2 = across(plus_1, [(dec(s - 1), dec(s)) for s in upper])
    minus_3 = across(minus_2, [(dec(s + 1), dec(s)) for s in lower])
    window = [plus_2, plus_1, at_home, minus_1, minus_2, minus_3]

    first_block = shard_index - REACH_LOW
    window_blocks = first_block + jnp.arange(WINDOW, dtype=jnp.int32)
    enc_segs = segment_of(window_blocks, enc_counts, count)
    segment = segment_of(jnp.reshape(shard_index, (1,)), dec_counts, count)[0]
    enc_starts = jnp.cumsum(enc_counts) - enc_counts
    start_block = jnp.clip(enc_starts[segment] - first_block, 0, WINDOW - ENC_MOST).astype(jnp.int32)
    slice_segs = lax.dynamic_slice_in_dim(enc_segs, start_block, ENC_MOST)
    allowed_keys = jnp.repeat(slice_segs == segment, BLOCK)

    def decoder_work(operands):
        own, pieces = operands
        return attention_block(jnp.reshape(start_block, (1,)), head_gains, own, pieces, allowed_keys)

    def encoder_rest(operands):
        own, pieces = operands
        zeros = jnp.zeros_like(own)
        return (zeros, (zeros,) * WINDOW, jnp.zeros((2, head_count), jnp.float32))

    produced, grads, terms = lax.cond(
        phase_index == 1, decoder_work, encoder_rest, (local_pair, window)
    )

    def added(a, b):
        return (a.astype(jnp.float32) + b.astype(jnp.float32)).astype(jnp.bfloat16)

    back_minus = across(grads[0], [(dec(s + 1), dec(s)) for s in lower])
    back_plus = across(grads[5], [(dec(s - 1), dec(s)) for s in upper])
    minus_sum = across(added(back_minus, grads[1]), [(dec(s + 1), enc(s)) for s in lower])
    back_plus = across(added(back_plus, grads[4]), [(dec(s - 1), dec(s)) for s in upper])
    plus_sum = across(added(back_plus, grads[3]), [(dec(s - 1), enc(s)) for s in upper])
    own_sum = across(grads[2], [(dec(s), enc(s)) for s in range(count)])
    returned = (
        own_sum.astype(jnp.float32) + minus_sum.astype(jnp.float32) + plus_sum.astype(jnp.float32)
    ).astype(jnp.bfloat16)

    token_total = tok_dev * count * lax.axis_size("dp")
    summed = butterfly_sum(butterfly_sum(butterfly_sum(terms, "phase"), "dp"), "seq")
    chosen = lax.dynamic_index_in_dim(summed, phase_index, 0, keepdims=False)
    scale = jnp.where(phase_index == 0, head_gains[1], 1.0) * math.sqrt(token_total)
    gain_total = chosen / scale
    result = jnp.where(phase_index == 0, returned, produced)[None]
    return (result, gain_total[None])


def solution(mesh):
    return jax.shard_map(
        local,
        mesh=mesh,
        in_specs=(P("phase", None, ("dp", "seq"), None), P(), P("dp", None, None)),
        out_specs=(P("phase", None, ("dp", "seq"), None), P("phase", None)),
        check_vma=False,
    )
```

```python
import math

import jax
import jax.numpy as jnp
from jax import lax
from jax.experimental import pallas as pl
from jax.experimental.pallas import tpu as pltpu
from jax.sharding import PartitionSpec as P

BLOCK = 128
ENC_MOST = 4
REACH_LOW = 2
REACH_HIGH = 3
WINDOW = REACH_LOW + REACH_HIGH + 1

masked_score = -1e30


def attention_kernel(start_ref, gains_ref, own_ref, *refs):
    window_refs = refs[:WINDOW]
    allow_ref = refs[WINDOW]
    out_ref = refs[WINDOW + 1]
    grad_refs = refs[WINDOW + 2 : 2 * WINDOW + 2]
    gain_ref = refs[2 * WINDOW + 2]
    pair = pl.program_id(0)
    start = start_ref[0]
    width = own_ref.shape[2]
    half = width // 2
    inv_root = 1.0 / math.sqrt(half)
    q = own_ref[0]
    do = own_ref[1]
    blocks = [ref[...] for ref in window_refs]

    def pick(slot):
        chosen = blocks[slot + WINDOW - ENC_MOST]
        for shift in range(WINDOW - ENC_MOST - 1, -1, -1):
            chosen = jnp.where(start == shift, blocks[slot + shift], chosen)
        return chosen

    slots = [pick(slot) for slot in range(ENC_MOST)]
    k = jnp.concatenate([piece[0] for piece in slots], axis=0)
    v = jnp.concatenate([piece[1] for piece in slots], axis=0)
    allowed = allow_ref[...] > 0
    lane = lax.broadcasted_iota(jnp.int32, (1, width), 1)
    first = lane < half
    heads = []
    att_parts = []
    for j in range(2):
        head = pair * 2 + j
        g_logit = gains_ref[0, head]
        g_value = gains_ref[1, head]
        mine = first if j == 0 else jnp.logical_not(first)
        q_h = jnp.where(mine, q, jnp.zeros_like(q))
        raw = lax.dot_general(q_h, k, (((1,), (1,)), ((), ())), preferred_element_type=jnp.float32) * inv_root
        logits = jnp.where(allowed, g_logit * raw, masked_score)
        top = jnp.max(logits, axis=1, keepdims=True)
        lifted = jnp.exp(logits - top)
        chances = lifted / jnp.sum(lifted, axis=1, keepdims=True)
        p_low = chances.astype(jnp.bfloat16)
        att_parts.append(jnp.dot(p_low, v, preferred_element_type=jnp.float32) * g_value)
        heads.append((g_logit, g_value, mine, raw, chances, p_low))
    attended = jnp.where(first, att_parts[0], att_parts[1]).astype(jnp.bfloat16)
    out_ref[0] = attended
    prod = do.astype(jnp.float32) * attended.astype(jnp.float32)
    dq_parts, dk_parts, dv_parts, logit_terms = [], [], [], []
    for g_logit, g_value, mine, raw, chances, p_low in heads:
        do_h = jnp.where(mine, do, jnp.zeros_like(do))
        slope = lax.dot_general(do_h, v, (((1,), (1,)), ((), ())), preferred_element_type=jnp.float32) * g_value
        carried = jnp.sum(jnp.where(mine, prod, 0.0), axis=1, keepdims=True)
        score_grad = chances * (slope - carried)
        score_low = score_grad.astype(jnp.bfloat16)
        factor = g_logit * inv_root
        dq_parts.append(jnp.dot(score_low, k, preferred_element_type=jnp.float32) * factor)
        dk_parts.append(lax.dot_general(score_low, q, (((0,), (0,)), ((), ())), preferred_element_type=jnp.float32) * factor)
        dv_parts.append(lax.dot_general(p_low, do, (((0,), (0,)), ((), ())), preferred_element_type=jnp.float32) * g_value)
        logit_terms.append(jnp.sum(score_grad * raw))
    out_ref[1] = jnp.where(first, dq_parts[0], dq_parts[1]).astype(jnp.bfloat16)
    key_grad = jnp.where(first, dk_parts[0], dk_parts[1]).astype(jnp.bfloat16)
    value_grad = jnp.where(first, dv_parts[0], dv_parts[1]).astype(jnp.bfloat16)
    value_prod = v.astype(jnp.float32) * value_grad.astype(jnp.float32)
    value_terms = [jnp.sum(jnp.where(first, value_prod, 0.0)), jnp.sum(jnp.where(first, 0.0, value_prod))]
    zero_block = jnp.zeros((BLOCK, width), jnp.bfloat16)
    for position in range(WINDOW):
        key_block = zero_block
        value_block = zero_block
        for slot in range(ENC_MOST):
            if 0 <= position - slot <= WINDOW - ENC_MOST:
                rows = slice(slot * BLOCK, (slot + 1) * BLOCK)
                key_block = jnp.where(start == position - slot, key_grad[rows], key_block)
                value_block = jnp.where(start == position - slot, value_grad[rows], value_block)
        grad_refs[position][0] = key_block
        grad_refs[position][1] = value_block
    glane = lax.broadcasted_iota(jnp.int32, gain_ref.shape, 2)
    terms = value_terms + logit_terms
    packed = jnp.zeros(gain_ref.shape, jnp.float32)
    for index, term in enumerate(terms):
        packed = jnp.where(glane == index, term, packed)
    gain_ref[...] = packed


def attention_block(start, head_gains, own, window, allowed_keys):
    _, rows, inner = own.shape
    keys = ENC_MOST * BLOCK
    head_count = head_gains.shape[1]
    width = 2 * (inner // head_count)
    pairs = inner // width
    block_spec = pl.BlockSpec((2, rows, width), lambda i, s, g: (0, 0, i))
    grid_spec = pltpu.PrefetchScalarGridSpec(
        num_scalar_prefetch=2,
        grid=(pairs,),
        in_specs=[block_spec] * (WINDOW + 1) + [pl.BlockSpec((1, keys), lambda i, s, g: (0, 0))],
        out_specs=[block_spec] * (WINDOW + 1) + [pl.BlockSpec((1, 8, 128), lambda i, s, g: (i, 0, 0))],
    )
    flops = 2 * rows * keys * width * 6 * pairs * 2
    cost = pl.CostEstimate(
        flops=flops,
        transcendentals=rows * keys * head_count,
        bytes_accessed=2 * 2 * rows * inner * (2 * WINDOW + 2),
    )
    outs = pl.pallas_call(
        attention_kernel,
        grid_spec=grid_spec,
        out_shape=[jax.ShapeDtypeStruct(own.shape, jnp.bfloat16)] * (WINDOW + 1)
        + [jax.ShapeDtypeStruct((pairs, 8, 128), jnp.float32)],
        cost_estimate=cost,
    )(start, head_gains, own, *window, allowed_keys.astype(jnp.int32)[None, :])
    produced = outs[0]
    grads = tuple(outs[1 : WINDOW + 1])
    packed = outs[WINDOW + 1]
    terms = jnp.stack([packed[:, 0, 0:2].reshape(-1), packed[:, 0, 2:4].reshape(-1)])
    return produced, grads, terms


def exchange_add(value, axis, stride):
    count = lax.axis_size(axis)
    return value + lax.ppermute(value, axis, [(i, i ^ stride) for i in range(count)])


def segment_of(block_ids, block_sizes, block_total):
    starts = jnp.cumsum(block_sizes) - block_sizes
    found = jnp.sum((starts[None, :] <= block_ids[:, None]).astype(jnp.int32), axis=1) - 1
    inside = jnp.logical_and(block_ids >= 0, block_ids < block_total)
    return jnp.where(inside, found, -1)


def local(sections, head_gains, block_counts):
    phase_index = lax.axis_index("phase")
    shard_index = lax.axis_index("seq")
    count = lax.axis_size("seq")
    local_pair = sections[0]
    tok_dev = local_pair.shape[1]
    head_count = head_gains.shape[1]
    enc_counts = block_counts[0, 0]
    dec_counts = block_counts[0, 1]

    def enc(s):
        return s

    def dec(s):
        return count + s

    def across(value, pairs):
        return lax.ppermute(value, ("phase", "seq"), pairs)

    lower = range(count - 1)
    upper = range(1, count)
    at_home = across(local_pair, [(enc(s), dec(s)) for s in range(count)])
    minus_1 = across(local_pair, [(enc(s + 1), dec(s)) for s in lower])
    plus_1 = across(local_pair, [(enc(s - 1), dec(s)) for s in upper])
    minus_2 = across(minus_1, [(dec(s + 1), dec(s)) for s in lower])
    plus_2 = across(plus_1, [(dec(s - 1), dec(s)) for s in upper])
    minus_3 = across(minus_2, [(dec(s + 1), dec(s)) for s in lower])
    window = [plus_2, plus_1, at_home, minus_1, minus_2, minus_3]

    first_block = shard_index - REACH_LOW
    window_blocks = first_block + jnp.arange(WINDOW, dtype=jnp.int32)
    enc_segs = segment_of(window_blocks, enc_counts, count)
    segment = segment_of(jnp.reshape(shard_index, (1,)), dec_counts, count)[0]
    enc_starts = jnp.cumsum(enc_counts) - enc_counts
    start_block = jnp.clip(enc_starts[segment] - first_block, 0, WINDOW - ENC_MOST).astype(jnp.int32)
    slice_segs = lax.dynamic_slice_in_dim(enc_segs, start_block, ENC_MOST)
    allowed_keys = jnp.repeat(slice_segs == segment, BLOCK)

    def decoder_work(operands):
        own, pieces = operands
        return attention_block(jnp.reshape(start_block, (1,)), head_gains, own, pieces, allowed_keys)

    def encoder_rest(operands):
        own, pieces = operands
        zeros = jnp.zeros_like(own)
        return (zeros, (zeros,) * WINDOW, jnp.zeros((2, head_count), jnp.float32))

    produced, grads, terms = lax.cond(
        phase_index == 1, decoder_work, encoder_rest, (local_pair, window)
    )

    def added(a, b):
        return (a.astype(jnp.float32) + b.astype(jnp.float32)).astype(jnp.bfloat16)

    token_total = tok_dev * count * lax.axis_size("dp")
    summed = exchange_add(terms, "phase", 1)
    back_minus = across(grads[0], [(dec(s + 1), dec(s)) for s in lower])
    back_plus = across(grads[5], [(dec(s - 1), dec(s)) for s in upper])
    own_sum = across(grads[2], [(dec(s), enc(s)) for s in range(count)])
    summed = exchange_add(exchange_add(summed, "dp", 1), "dp", 2)
    summed, back_minus, back_plus = lax.optimization_barrier((summed, back_minus, back_plus))
    minus_sum = across(added(back_minus, grads[1]), [(dec(s + 1), enc(s)) for s in lower])
    back_plus = across(added(back_plus, grads[4]), [(dec(s - 1), dec(s)) for s in upper])
    summed = exchange_add(exchange_add(exchange_add(summed, "dp", 4), "seq", 1), "seq", 2)
    summed, back_plus = lax.optimization_barrier((summed, back_plus))
    plus_sum = across(added(back_plus, grads[3]), [(dec(s - 1), enc(s)) for s in upper])
    summed = exchange_add(exchange_add(summed, "seq", 4), "seq", 8)
    returned = (
        own_sum.astype(jnp.float32) + minus_sum.astype(jnp.float32) + plus_sum.astype(jnp.float32)
    ).astype(jnp.bfloat16)
    chosen = lax.dynamic_index_in_dim(summed, phase_index, 0, keepdims=False)
    scale = jnp.where(phase_index == 0, head_gains[1], 1.0) * math.sqrt(token_total)
    gain_total = chosen / scale
    result = jnp.where(phase_index == 0, returned, produced)[None]
    return (result, gain_total[None])


def solution(mesh):
    return jax.shard_map(
        local,
        mesh=mesh,
        in_specs=(P("phase", None, ("dp", "seq"), None), P(), P("dp", None, None)),
        out_specs=(P("phase", None, ("dp", "seq"), None), P("phase", None)),
        check_vma=False,
    )
```

```python
import math

import jax
import jax.numpy as jnp
from jax import lax
from jax.experimental import pallas as pl
from jax.experimental.pallas import tpu as pltpu
from jax.sharding import PartitionSpec as P

BLOCK = 128
ENC_MOST = 4
REACH_LOW = 2
REACH_HIGH = 3
WINDOW = REACH_LOW + REACH_HIGH + 1
RING = 8

masked_score = -1e30


def attention_kernel(start_ref, gains_ref, own_ref, *refs):
    window_refs = refs[:WINDOW]
    allow_ref = refs[WINDOW]
    out_ref = refs[WINDOW + 1]
    grad_refs = refs[WINDOW + 2 : 2 * WINDOW + 2]
    gain_ref = refs[2 * WINDOW + 2]
    pair = pl.program_id(0)
    start = start_ref[0]
    width = own_ref.shape[2]
    half = width // 2
    inv_root = 1.0 / math.sqrt(half)
    q = own_ref[0]
    do = own_ref[1]
    blocks = [ref[...] for ref in window_refs]

    def pick(slot):
        chosen = blocks[slot + WINDOW - ENC_MOST]
        for shift in range(WINDOW - ENC_MOST - 1, -1, -1):
            chosen = jnp.where(start == shift, blocks[slot + shift], chosen)
        return chosen

    slots = [pick(slot) for slot in range(ENC_MOST)]
    k = jnp.concatenate([piece[0] for piece in slots], axis=0)
    v = jnp.concatenate([piece[1] for piece in slots], axis=0)
    allowed = allow_ref[...] > 0
    lane = lax.broadcasted_iota(jnp.int32, (1, width), 1)
    first = lane < half
    heads = []
    att_parts = []
    for j in range(2):
        head = pair * 2 + j
        g_logit = gains_ref[0, head]
        g_value = gains_ref[1, head]
        mine = first if j == 0 else jnp.logical_not(first)
        q_h = jnp.where(mine, q, jnp.zeros_like(q))
        raw = lax.dot_general(q_h, k, (((1,), (1,)), ((), ())), preferred_element_type=jnp.float32) * inv_root
        logits = jnp.where(allowed, g_logit * raw, masked_score)
        top = jnp.max(logits, axis=1, keepdims=True)
        lifted = jnp.exp(logits - top)
        chances = lifted / jnp.sum(lifted, axis=1, keepdims=True)
        p_low = chances.astype(jnp.bfloat16)
        att_parts.append(jnp.dot(p_low, v, preferred_element_type=jnp.float32) * g_value)
        heads.append((g_logit, g_value, mine, raw, chances, p_low))
    attended = jnp.where(first, att_parts[0], att_parts[1]).astype(jnp.bfloat16)
    out_ref[0] = attended
    prod = do.astype(jnp.float32) * attended.astype(jnp.float32)
    dq_parts, dk_parts, dv_parts, logit_terms = [], [], [], []
    for g_logit, g_value, mine, raw, chances, p_low in heads:
        do_h = jnp.where(mine, do, jnp.zeros_like(do))
        slope = lax.dot_general(do_h, v, (((1,), (1,)), ((), ())), preferred_element_type=jnp.float32) * g_value
        carried = jnp.sum(jnp.where(mine, prod, 0.0), axis=1, keepdims=True)
        score_grad = chances * (slope - carried)
        score_low = score_grad.astype(jnp.bfloat16)
        factor = g_logit * inv_root
        dq_parts.append(jnp.dot(score_low, k, preferred_element_type=jnp.float32) * factor)
        dk_parts.append(lax.dot_general(score_low, q, (((0,), (0,)), ((), ())), preferred_element_type=jnp.float32) * factor)
        dv_parts.append(lax.dot_general(p_low, do, (((0,), (0,)), ((), ())), preferred_element_type=jnp.float32) * g_value)
        logit_terms.append(jnp.sum(score_grad * raw))
    out_ref[1] = jnp.where(first, dq_parts[0], dq_parts[1]).astype(jnp.bfloat16)
    key_grad = jnp.where(first, dk_parts[0], dk_parts[1]).astype(jnp.bfloat16)
    value_grad = jnp.where(first, dv_parts[0], dv_parts[1]).astype(jnp.bfloat16)
    value_prod = v.astype(jnp.float32) * value_grad.astype(jnp.float32)
    value_terms = [jnp.sum(jnp.where(first, value_prod, 0.0)), jnp.sum(jnp.where(first, 0.0, value_prod))]
    zero_block = jnp.zeros((BLOCK, width), jnp.bfloat16)
    for position in range(WINDOW):
        key_block = zero_block
        value_block = zero_block
        for slot in range(ENC_MOST):
            if 0 <= position - slot <= WINDOW - ENC_MOST:
                rows = slice(slot * BLOCK, (slot + 1) * BLOCK)
                key_block = jnp.where(start == position - slot, key_grad[rows], key_block)
                value_block = jnp.where(start == position - slot, value_grad[rows], value_block)
        grad_refs[position][0] = key_block
        grad_refs[position][1] = value_block
    glane = lax.broadcasted_iota(jnp.int32, gain_ref.shape, 2)
    terms = value_terms + logit_terms
    packed = jnp.zeros(gain_ref.shape, jnp.float32)
    for index, term in enumerate(terms):
        packed = jnp.where(glane == index, term, packed)
    gain_ref[...] = packed


def attention_block(start, head_gains, own, window, allowed_keys):
    _, rows, inner = own.shape
    keys = ENC_MOST * BLOCK
    head_count = head_gains.shape[1]
    width = 2 * (inner // head_count)
    pairs = inner // width
    block_spec = pl.BlockSpec((2, rows, width), lambda i, s, g: (0, 0, i))
    grid_spec = pltpu.PrefetchScalarGridSpec(
        num_scalar_prefetch=2,
        grid=(pairs,),
        in_specs=[block_spec] * (WINDOW + 1) + [pl.BlockSpec((1, keys), lambda i, s, g: (0, 0))],
        out_specs=[block_spec] * (WINDOW + 1) + [pl.BlockSpec((1, 8, 128), lambda i, s, g: (i, 0, 0))],
    )
    flops = 2 * rows * keys * width * 6 * pairs * 2
    cost = pl.CostEstimate(
        flops=flops,
        transcendentals=rows * keys * head_count,
        bytes_accessed=2 * 2 * rows * inner * (2 * WINDOW + 2),
    )
    outs = pl.pallas_call(
        attention_kernel,
        grid_spec=grid_spec,
        out_shape=[jax.ShapeDtypeStruct(own.shape, jnp.bfloat16)] * (WINDOW + 1)
        + [jax.ShapeDtypeStruct((pairs, 8, 128), jnp.float32)],
        cost_estimate=cost,
    )(start, head_gains, own, *window, allowed_keys.astype(jnp.int32)[None, :])
    produced = outs[0]
    grads = tuple(outs[1 : WINDOW + 1])
    packed = outs[WINDOW + 1]
    terms = jnp.stack([packed[:, 0, 0:2].reshape(-1), packed[:, 0, 2:4].reshape(-1)])
    return produced, grads, terms


def ring_shift(value, steps):
    count = lax.axis_size("seq")
    pairs = []
    for source in range(count):
        base = source - source % RING
        pairs.append((source, base + (source - steps) % RING))
    return lax.ppermute(value, "seq", pairs)


def ring_total(value, shard_index):
    gathered = value[None]
    gathered = jnp.concatenate([gathered, ring_shift(gathered, 1)], axis=0)
    gathered = jnp.concatenate([gathered, ring_shift(gathered, 2)], axis=0)
    while gathered.shape[0] < RING:
        have = gathered.shape[0]
        gathered = jnp.concatenate([gathered, ring_shift(gathered, 2)[have - 2 : have]], axis=0)
    ordered = jnp.roll(gathered, shard_index % RING, axis=0)
    total = ordered[0]
    for index in range(1, RING):
        total = total + ordered[index]
    return total


def exchange_add(value, axis, stride):
    count = lax.axis_size(axis)
    return value + lax.ppermute(value, axis, [(i, i ^ stride) for i in range(count)])


def segment_of(block_ids, block_sizes, block_total):
    starts = jnp.cumsum(block_sizes) - block_sizes
    found = jnp.sum((starts[None, :] <= block_ids[:, None]).astype(jnp.int32), axis=1) - 1
    inside = jnp.logical_and(block_ids >= 0, block_ids < block_total)
    return jnp.where(inside, found, -1)


def local(sections, head_gains, block_counts):
    phase_index = lax.axis_index("phase")
    shard_index = lax.axis_index("seq")
    count = lax.axis_size("seq")
    local_pair = sections[0]
    tok_dev = local_pair.shape[1]
    head_count = head_gains.shape[1]
    enc_counts = block_counts[0, 0]
    dec_counts = block_counts[0, 1]

    def enc(s):
        return s

    def dec(s):
        return count + s

    def across(value, pairs):
        return lax.ppermute(value, ("phase", "seq"), pairs)

    lower = range(count - 1)
    upper = range(1, count)
    at_home = across(local_pair, [(enc(s), dec(s)) for s in range(count)])
    minus_1 = across(local_pair, [(enc(s + 1), dec(s)) for s in lower])
    plus_1 = across(local_pair, [(enc(s - 1), dec(s)) for s in upper])
    minus_2 = across(minus_1, [(dec(s + 1), dec(s)) for s in lower])
    plus_2 = across(plus_1, [(dec(s - 1), dec(s)) for s in upper])
    minus_3 = across(minus_2, [(dec(s + 1), dec(s)) for s in lower])
    window = [plus_2, plus_1, at_home, minus_1, minus_2, minus_3]

    first_block = shard_index - REACH_LOW
    window_blocks = first_block + jnp.arange(WINDOW, dtype=jnp.int32)
    enc_segs = segment_of(window_blocks, enc_counts, count)
    segment = segment_of(jnp.reshape(shard_index, (1,)), dec_counts, count)[0]
    enc_starts = jnp.cumsum(enc_counts) - enc_counts
    start_block = jnp.clip(enc_starts[segment] - first_block, 0, WINDOW - ENC_MOST).astype(jnp.int32)
    slice_segs = lax.dynamic_slice_in_dim(enc_segs, start_block, ENC_MOST)
    allowed_keys = jnp.repeat(slice_segs == segment, BLOCK)

    def decoder_work(operands):
        own, pieces = operands
        return attention_block(jnp.reshape(start_block, (1,)), head_gains, own, pieces, allowed_keys)

    def encoder_rest(operands):
        own, pieces = operands
        zeros = jnp.zeros_like(own)
        return (zeros, (zeros,) * WINDOW, jnp.zeros((2, head_count), jnp.float32))

    produced, grads, terms = lax.cond(
        phase_index == 1, decoder_work, encoder_rest, (local_pair, window)
    )

    def added(a, b):
        return (a.astype(jnp.float32) + b.astype(jnp.float32)).astype(jnp.bfloat16)

    token_total = tok_dev * count * lax.axis_size("dp")
    summed = exchange_add(terms, "phase", 1)
    back_minus = across(grads[0], [(dec(s + 1), dec(s)) for s in lower])
    back_plus = across(grads[5], [(dec(s - 1), dec(s)) for s in upper])
    own_sum = across(grads[2], [(dec(s), enc(s)) for s in range(count)])
    summed = exchange_add(exchange_add(exchange_add(summed, "dp", 1), "dp", 2), "dp", 4)
    summed, back_minus, back_plus = lax.optimization_barrier((summed, back_minus, back_plus))
    minus_sum = across(added(back_minus, grads[1]), [(dec(s + 1), enc(s)) for s in lower])
    back_plus = across(added(back_plus, grads[4]), [(dec(s - 1), dec(s)) for s in upper])
    summed = exchange_add(summed, "seq", RING)
    summed, back_plus = lax.optimization_barrier((summed, back_plus))
    plus_sum = across(added(back_plus, grads[3]), [(dec(s - 1), enc(s)) for s in upper])
    summed = ring_total(summed, shard_index)
    returned = (
        own_sum.astype(jnp.float32) + minus_sum.astype(jnp.float32) + plus_sum.astype(jnp.float32)
    ).astype(jnp.bfloat16)
    chosen = lax.dynamic_index_in_dim(summed, phase_index, 0, keepdims=False)
    scale = jnp.where(phase_index == 0, head_gains[1], 1.0) * math.sqrt(token_total)
    gain_total = chosen / scale
    result = jnp.where(phase_index == 0, returned, produced)[None]
    return (result, gain_total[None])


def solution(mesh):
    return jax.shard_map(
        local,
        mesh=mesh,
        in_specs=(P("phase", None, ("dp", "seq"), None), P(), P("dp", None, None)),
        out_specs=(P("phase", None, ("dp", "seq"), None), P("phase", None)),
        check_vma=False,
    )
```

```python
import math

import jax
import jax.numpy as jnp
from jax import lax
from jax.experimental import pallas as pl
from jax.experimental.pallas import tpu as pltpu
from jax.sharding import PartitionSpec as P


BLOCK = 128
ENC_MOST = 4
REACH_LOW = 2
REACH_HIGH = 3
WINDOW = REACH_LOW + REACH_HIGH + 1
RING = 8

masked_score = -1e30


def attention_kernel(start_ref, gains_ref, own_ref, *refs):
    window_refs = refs[:WINDOW]
    allow_ref = refs[WINDOW]
    out_ref = refs[WINDOW + 1]
    grad_refs = refs[WINDOW + 2 : 2 * WINDOW + 2]
    gain_ref = refs[2 * WINDOW + 2]
    pair = pl.program_id(0)
    start = start_ref[0]
    width = own_ref.shape[2]
    half = width // 2
    inv_root = 1.0 / math.sqrt(half)
    q = own_ref[0]
    do = own_ref[1]
    blocks = [ref[...] for ref in window_refs]

    def pick(slot):
        chosen = blocks[slot + WINDOW - ENC_MOST]
        for shift in range(WINDOW - ENC_MOST - 1, -1, -1):
            chosen = jnp.where(start == shift, blocks[slot + shift], chosen)
        return chosen

    slots = [pick(slot) for slot in range(ENC_MOST)]
    k = jnp.concatenate([piece[0] for piece in slots], axis=0)
    v = jnp.concatenate([piece[1] for piece in slots], axis=0)
    allowed = allow_ref[...] > 0
    lane = lax.broadcasted_iota(jnp.int32, (1, width), 1)
    first = lane < half
    heads = []
    att_parts = []
    for j in range(2):
        head = pair * 2 + j
        g_logit = gains_ref[0, head]
        g_value = gains_ref[1, head]
        mine = first if j == 0 else jnp.logical_not(first)
        q_h = jnp.where(mine, q, jnp.zeros_like(q))
        raw = lax.dot_general(q_h, k, (((1,), (1,)), ((), ())), preferred_element_type=jnp.float32) * inv_root
        logits = jnp.where(allowed, g_logit * raw, masked_score)
        top = jnp.max(logits, axis=1, keepdims=True)
        lifted = jnp.exp(logits - top)
        chances = lifted / jnp.sum(lifted, axis=1, keepdims=True)
        p_low = chances.astype(jnp.bfloat16)
        att_parts.append(jnp.dot(p_low, v, preferred_element_type=jnp.float32) * g_value)
        heads.append((g_logit, g_value, mine, raw, chances, p_low))
    attended = jnp.where(first, att_parts[0], att_parts[1]).astype(jnp.bfloat16)
    out_ref[0] = attended
    prod = do.astype(jnp.float32) * attended.astype(jnp.float32)
    dq_parts, dk_parts, dv_parts, logit_terms = [], [], [], []
    for g_logit, g_value, mine, raw, chances, p_low in heads:
        do_h = jnp.where(mine, do, jnp.zeros_like(do))
        slope = lax.dot_general(do_h, v, (((1,), (1,)), ((), ())), preferred_element_type=jnp.float32) * g_value
        carried = jnp.sum(jnp.where(mine, prod, 0.0), axis=1, keepdims=True)
        score_grad = chances * (slope - carried)
        score_low = score_grad.astype(jnp.bfloat16)
        factor = g_logit * inv_root
        dq_parts.append(jnp.dot(score_low, k, preferred_element_type=jnp.float32) * factor)
        dk_parts.append(lax.dot_general(score_low, q, (((0,), (0,)), ((), ())), preferred_element_type=jnp.float32) * factor)
        dv_parts.append(lax.dot_general(p_low, do, (((0,), (0,)), ((), ())), preferred_element_type=jnp.float32) * g_value)
        logit_terms.append(jnp.sum(score_grad * raw))
    out_ref[1] = jnp.where(first, dq_parts[0], dq_parts[1]).astype(jnp.bfloat16)
    key_grad = jnp.where(first, dk_parts[0], dk_parts[1]).astype(jnp.bfloat16)
    value_grad = jnp.where(first, dv_parts[0], dv_parts[1]).astype(jnp.bfloat16)
    value_prod = v.astype(jnp.float32) * value_grad.astype(jnp.float32)
    value_terms = [jnp.sum(jnp.where(first, value_prod, 0.0)), jnp.sum(jnp.where(first, 0.0, value_prod))]
    zero_block = jnp.zeros((BLOCK, width), jnp.bfloat16)
    for position in range(WINDOW):
        key_block = zero_block
        value_block = zero_block
        for slot in range(ENC_MOST):
            if 0 <= position - slot <= WINDOW - ENC_MOST:
                rows = slice(slot * BLOCK, (slot + 1) * BLOCK)
                key_block = jnp.where(start == position - slot, key_grad[rows], key_block)
                value_block = jnp.where(start == position - slot, value_grad[rows], value_block)
        grad_refs[position][0] = key_block
        grad_refs[position][1] = value_block
    glane = lax.broadcasted_iota(jnp.int32, gain_ref.shape, 2)
    terms = value_terms + logit_terms
    packed = jnp.zeros(gain_ref.shape, jnp.float32)
    for index, term in enumerate(terms):
        packed = jnp.where(glane == index, term, packed)
    gain_ref[...] = packed


def attention_block(start, head_gains, own, window, allowed_keys):
    _, rows, inner = own.shape
    keys = ENC_MOST * BLOCK
    head_count = head_gains.shape[1]
    width = 2 * (inner // head_count)
    pairs = inner // width
    block_spec = pl.BlockSpec((2, rows, width), lambda i, s, g: (0, 0, i))
    grid_spec = pltpu.PrefetchScalarGridSpec(
        num_scalar_prefetch=2,
        grid=(pairs,),
        in_specs=[block_spec] * (WINDOW + 1) + [pl.BlockSpec((1, keys), lambda i, s, g: (0, 0))],
        out_specs=[block_spec] * (WINDOW + 1) + [pl.BlockSpec((1, 8, 128), lambda i, s, g: (i, 0, 0))],
    )
    flops = 2 * rows * keys * width * 6 * pairs * 2
    cost = pl.CostEstimate(
        flops=flops,
        transcendentals=rows * keys * head_count,
        bytes_accessed=2 * 2 * rows * inner * (2 * WINDOW + 2),
    )
    outs = pl.pallas_call(
        attention_kernel,
        grid_spec=grid_spec,
        out_shape=[jax.ShapeDtypeStruct(own.shape, jnp.bfloat16)] * (WINDOW + 1)
        + [jax.ShapeDtypeStruct((pairs, 8, 128), jnp.float32)],
        cost_estimate=cost,
    )(start, head_gains, own, *window, allowed_keys.astype(jnp.int32)[None, :])
    produced = outs[0]
    grads = tuple(outs[1 : WINDOW + 1])
    packed = outs[WINDOW + 1]
    terms = jnp.stack([packed[:, 0, 0:2].reshape(-1), packed[:, 0, 2:4].reshape(-1)])
    return produced, grads, terms


def ring_shift(value, steps):
    count = lax.axis_size("seq")
    pairs = []
    for source in range(count):
        base = source - source % RING
        pairs.append((source, base + (source - steps) % RING))
    return lax.ppermute(value, "seq", pairs)


def ring_total(value, shard_index):
    gathered = value[None]
    gathered = jnp.concatenate([gathered, ring_shift(gathered, 1)], axis=0)
    gathered = jnp.concatenate([gathered, ring_shift(gathered, 2)], axis=0)
    while gathered.shape[0] < RING:
        have = gathered.shape[0]
        gathered = jnp.concatenate([gathered, ring_shift(gathered, 2)[have - 2 : have]], axis=0)
    ordered = jnp.roll(gathered, shard_index % RING, axis=0)
    total = ordered[0]
    for index in range(1, RING):
        total = total + ordered[index]
    return total


def exchange_add(value, axis, stride):
    count = lax.axis_size(axis)
    return value + lax.ppermute(value, axis, [(i, i ^ stride) for i in range(count)])


def segment_of(block_ids, block_sizes, block_total):
    starts = jnp.cumsum(block_sizes) - block_sizes
    found = jnp.sum((starts[None, :] <= block_ids[:, None]).astype(jnp.int32), axis=1) - 1
    inside = jnp.logical_and(block_ids >= 0, block_ids < block_total)
    return jnp.where(inside, found, -1)


def local_body(sections, head_gains, block_counts):
    phase_index = lax.axis_index("phase")
    shard_index = lax.axis_index("seq")
    count = lax.axis_size("seq")
    local_pair = sections[0]
    tok_dev = local_pair.shape[1]
    head_count = head_gains.shape[1]
    enc_counts = block_counts[0, 0]
    dec_counts = block_counts[0, 1]

    def dec(s):
        return count + s

    def across(value, pairs):
        return lax.ppermute(value, ("phase", "seq"), pairs)

    lower = range(count - 1)
    upper = range(1, count)
    at_home = across(local_pair, [(s, dec(s)) for s in range(count)])
    minus_1 = across(local_pair, [(s + 1, dec(s)) for s in lower])
    plus_1 = across(local_pair, [(s - 1, dec(s)) for s in upper])
    minus_2 = across(minus_1, [(dec(s + 1), dec(s)) for s in lower])
    plus_2 = across(plus_1, [(dec(s - 1), dec(s)) for s in upper])
    minus_3 = across(minus_2, [(dec(s + 1), dec(s)) for s in lower])
    window = [plus_2, plus_1, at_home, minus_1, minus_2, minus_3]

    first_block = shard_index - REACH_LOW
    window_blocks = first_block + jnp.arange(WINDOW, dtype=jnp.int32)
    enc_segs = segment_of(window_blocks, enc_counts, count)
    segment = segment_of(jnp.reshape(shard_index, (1,)), dec_counts, count)[0]
    enc_starts = jnp.cumsum(enc_counts) - enc_counts
    start_block = jnp.clip(enc_starts[segment] - first_block, 0, WINDOW - ENC_MOST).astype(jnp.int32)
    slice_segs = lax.dynamic_slice_in_dim(enc_segs, start_block, ENC_MOST)
    allowed_keys = jnp.repeat(slice_segs == segment, BLOCK)

    def decoder_work(operands):
        own, pieces = operands
        return attention_block(jnp.reshape(start_block, (1,)), head_gains, own, pieces, allowed_keys)

    def encoder_rest(operands):
        own, _ = operands
        zeros = jnp.zeros_like(own)
        return (zeros, (zeros,) * WINDOW, jnp.zeros((2, head_count), jnp.float32))

    produced, grads, terms = lax.cond(
        phase_index == 1, decoder_work, encoder_rest, (local_pair, window)
    )

    def added(a, b):
        return (a.astype(jnp.float32) + b.astype(jnp.float32)).astype(jnp.bfloat16)

    token_total = tok_dev * count * lax.axis_size("dp")
    summed = exchange_add(terms, "phase", 1)
    back_minus = across(grads[0], [(dec(s + 1), dec(s)) for s in lower])
    back_plus = across(grads[5], [(dec(s - 1), dec(s)) for s in upper])
    own_sum = across(grads[2], [(dec(s), s) for s in range(count)])
    summed = exchange_add(exchange_add(exchange_add(summed, "dp", 1), "dp", 2), "dp", 4)
    summed, back_minus, back_plus = lax.optimization_barrier((summed, back_minus, back_plus))
    minus_sum = across(added(back_minus, grads[1]), [(dec(s + 1), s) for s in lower])
    back_plus = across(added(back_plus, grads[4]), [(dec(s - 1), dec(s)) for s in upper])
    summed = exchange_add(summed, "seq", RING)
    summed, back_plus = lax.optimization_barrier((summed, back_plus))
    plus_sum = across(added(back_plus, grads[3]), [(dec(s - 1), s) for s in upper])
    summed = ring_total(summed, shard_index)
    returned = (
        own_sum.astype(jnp.float32) + minus_sum.astype(jnp.float32) + plus_sum.astype(jnp.float32)
    ).astype(jnp.bfloat16)
    chosen = lax.dynamic_index_in_dim(summed, phase_index, 0, keepdims=False)
    scale = jnp.where(phase_index == 0, head_gains[1], 1.0) * math.sqrt(token_total)
    gain_total = chosen / scale
    result = jnp.where(phase_index == 0, returned, produced)[None]
    return (result, gain_total[None])


def solution(mesh):
    return jax.shard_map(
        local_body,
        mesh=mesh,
        in_specs=(P("phase", None, ("dp", "seq"), None), P(), P("dp", None, None)),
        out_specs=(P("phase", None, ("dp", "seq"), None), P("phase", None)),
        check_vma=False,
    )
```

```python
import math

import jax
import jax.numpy as jnp
from jax import lax
from jax.experimental import pallas as pl
from jax.experimental.pallas import tpu as pltpu
from jax.sharding import PartitionSpec as P


BLOCK = 128
ENC_MOST = 4
REACH_LOW = 2
REACH_HIGH = 3
WINDOW = REACH_LOW + REACH_HIGH + 1
RING = 8

masked_score = -1e30


def attention_kernel(start_ref, gains_ref, own_ref, *refs):
    window_refs = refs[:WINDOW]
    allow_ref = refs[WINDOW]
    out_ref = refs[WINDOW + 1]
    grad_refs = refs[WINDOW + 2 : 2 * WINDOW + 2]
    gain_ref = refs[2 * WINDOW + 2]
    pair = pl.program_id(0)
    start = start_ref[0]
    width = own_ref.shape[2]
    half = width // 2
    inv_root = 1.0 / math.sqrt(half)
    q = own_ref[0]
    do = own_ref[1]
    blocks = [ref[...] for ref in window_refs]

    def pick(slot):
        chosen = blocks[slot + WINDOW - ENC_MOST]
        for shift in range(WINDOW - ENC_MOST - 1, -1, -1):
            chosen = jnp.where(start == shift, blocks[slot + shift], chosen)
        return chosen

    slots = [pick(slot) for slot in range(ENC_MOST)]
    k = jnp.concatenate([piece[0] for piece in slots], axis=0)
    v = jnp.concatenate([piece[1] for piece in slots], axis=0)
    allowed = allow_ref[...] > 0
    lane = lax.broadcasted_iota(jnp.int32, (1, width), 1)
    first = lane < half
    heads = []
    att_parts = []
    for j in range(2):
        head = pair * 2 + j
        g_logit = gains_ref[0, head]
        g_value = gains_ref[1, head]
        mine = first if j == 0 else jnp.logical_not(first)
        q_h = jnp.where(mine, q, jnp.zeros_like(q))
        raw = lax.dot_general(q_h, k, (((1,), (1,)), ((), ())), preferred_element_type=jnp.float32)
        logits = jnp.where(allowed, (g_logit * inv_root) * raw, masked_score)
        top = jnp.max(logits, axis=1, keepdims=True)
        lifted = jnp.exp(logits - top)
        chances = lifted * (1.0 / jnp.sum(lifted, axis=1, keepdims=True))
        p_low = chances.astype(jnp.bfloat16)
        att_parts.append(jnp.dot(p_low, v, preferred_element_type=jnp.float32) * g_value)
        heads.append((g_logit, g_value, mine, raw, chances, p_low))
    attended = jnp.where(first, att_parts[0], att_parts[1]).astype(jnp.bfloat16)
    out_ref[0] = attended
    prod = do.astype(jnp.float32) * attended.astype(jnp.float32)
    dq_parts, dk_parts, dv_parts, logit_terms = [], [], [], []
    for g_logit, g_value, mine, raw, chances, p_low in heads:
        do_h = jnp.where(mine, do, jnp.zeros_like(do))
        slope = lax.dot_general(do_h, v, (((1,), (1,)), ((), ())), preferred_element_type=jnp.float32) * g_value
        carried = jnp.sum(jnp.where(mine, prod, 0.0), axis=1, keepdims=True)
        score_grad = chances * (slope - carried)
        score_low = score_grad.astype(jnp.bfloat16)
        factor = g_logit * inv_root
        dq_parts.append(jnp.dot(score_low, k, preferred_element_type=jnp.float32) * factor)
        dk_parts.append(lax.dot_general(score_low, q, (((0,), (0,)), ((), ())), preferred_element_type=jnp.float32) * factor)
        dv_parts.append(lax.dot_general(p_low, do, (((0,), (0,)), ((), ())), preferred_element_type=jnp.float32) * g_value)
        logit_terms.append(jnp.sum(score_grad * raw) * inv_root)
    out_ref[1] = jnp.where(first, dq_parts[0], dq_parts[1]).astype(jnp.bfloat16)
    key_grad = jnp.where(first, dk_parts[0], dk_parts[1]).astype(jnp.bfloat16)
    value_grad = jnp.where(first, dv_parts[0], dv_parts[1]).astype(jnp.bfloat16)
    value_prod = v.astype(jnp.float32) * value_grad.astype(jnp.float32)
    value_terms = [jnp.sum(jnp.where(first, value_prod, 0.0)), jnp.sum(jnp.where(first, 0.0, value_prod))]
    zero_block = jnp.zeros((BLOCK, width), jnp.bfloat16)
    for position in range(WINDOW):
        key_block = zero_block
        value_block = zero_block
        for slot in range(ENC_MOST):
            if 0 <= position - slot <= WINDOW - ENC_MOST:
                rows = slice(slot * BLOCK, (slot + 1) * BLOCK)
                key_block = jnp.where(start == position - slot, key_grad[rows], key_block)
                value_block = jnp.where(start == position - slot, value_grad[rows], value_block)
        grad_refs[position][0] = key_block
        grad_refs[position][1] = value_block
    glane = lax.broadcasted_iota(jnp.int32, gain_ref.shape, 2)
    terms = value_terms + logit_terms
    packed = jnp.zeros(gain_ref.shape, jnp.float32)
    for index, term in enumerate(terms):
        packed = jnp.where(glane == index, term, packed)
    gain_ref[...] = packed


def attention_block(start, head_gains, own, window, allowed_keys):
    _, rows, inner = own.shape
    keys = ENC_MOST * BLOCK
    head_count = head_gains.shape[1]
    width = 2 * (inner // head_count)
    pairs = inner // width
    block_spec = pl.BlockSpec((2, rows, width), lambda i, s, g: (0, 0, i))
    grid_spec = pltpu.PrefetchScalarGridSpec(
        num_scalar_prefetch=2,
        grid=(pairs,),
        in_specs=[block_spec] * (WINDOW + 1) + [pl.BlockSpec((1, keys), lambda i, s, g: (0, 0))],
        out_specs=[block_spec] * (WINDOW + 1) + [pl.BlockSpec((1, 8, 128), lambda i, s, g: (i, 0, 0))],
    )
    flops = 2 * rows * keys * width * 6 * pairs * 2
    cost = pl.CostEstimate(
        flops=flops,
        transcendentals=rows * keys * head_count,
        bytes_accessed=2 * 2 * rows * inner * (2 * WINDOW + 2),
    )
    outs = pl.pallas_call(
        attention_kernel,
        grid_spec=grid_spec,
        out_shape=[jax.ShapeDtypeStruct(own.shape, jnp.bfloat16)] * (WINDOW + 1)
        + [jax.ShapeDtypeStruct((pairs, 8, 128), jnp.float32)],
        cost_estimate=cost,
    )(start, head_gains, own, *window, allowed_keys.astype(jnp.int32)[None, :])
    produced = outs[0]
    grads = tuple(outs[1 : WINDOW + 1])
    packed = outs[WINDOW + 1]
    terms = jnp.stack([packed[:, 0, 0:2].reshape(-1), packed[:, 0, 2:4].reshape(-1)])
    return produced, grads, terms


def ring_shift(value, steps):
    count = lax.axis_size("seq")
    pairs = []
    for source in range(count):
        base = source - source % RING
        pairs.append((source, base + (source - steps) % RING))
    return lax.ppermute(value, "seq", pairs)


def ring_total(value, shard_index):
    gathered = value[None]
    gathered = jnp.concatenate([gathered, ring_shift(gathered, 1)], axis=0)
    gathered = jnp.concatenate([gathered, ring_shift(gathered, 2)], axis=0)
    while gathered.shape[0] < RING:
        have = gathered.shape[0]
        gathered = jnp.concatenate([gathered, ring_shift(gathered, 2)[have - 2 : have]], axis=0)
    ordered = jnp.roll(gathered, shard_index % RING, axis=0)
    total = ordered[0]
    for index in range(1, RING):
        total = total + ordered[index]
    return total


def exchange_add(value, axis, stride):
    count = lax.axis_size(axis)
    return value + lax.ppermute(value, axis, [(i, i ^ stride) for i in range(count)])


def segment_of(block_ids, block_sizes, block_total):
    starts = jnp.cumsum(block_sizes) - block_sizes
    found = jnp.sum((starts[None, :] <= block_ids[:, None]).astype(jnp.int32), axis=1) - 1
    inside = jnp.logical_and(block_ids >= 0, block_ids < block_total)
    return jnp.where(inside, found, -1)


def local_body(sections, head_gains, block_counts):
    phase_index = lax.axis_index("phase")
    shard_index = lax.axis_index("seq")
    count = lax.axis_size("seq")
    local_pair = sections[0]
    tok_dev = local_pair.shape[1]
    head_count = head_gains.shape[1]
    enc_counts = block_counts[0, 0]
    dec_counts = block_counts[0, 1]

    def dec(s):
        return count + s

    def across(value, pairs):
        return lax.ppermute(value, ("phase", "seq"), pairs)

    lower = range(count - 1)
    upper = range(1, count)
    at_home = across(local_pair, [(s, dec(s)) for s in range(count)])
    minus_1 = across(local_pair, [(s + 1, dec(s)) for s in lower])
    plus_1 = across(local_pair, [(s - 1, dec(s)) for s in upper])
    minus_2 = across(minus_1, [(dec(s + 1), dec(s)) for s in lower])
    plus_2 = across(plus_1, [(dec(s - 1), dec(s)) for s in upper])
    minus_3 = across(minus_2, [(dec(s + 1), dec(s)) for s in lower])
    window = [plus_2, plus_1, at_home, minus_1, minus_2, minus_3]

    first_block = shard_index - REACH_LOW
    window_blocks = first_block + jnp.arange(WINDOW, dtype=jnp.int32)
    enc_segs = segment_of(window_blocks, enc_counts, count)
    segment = segment_of(jnp.reshape(shard_index, (1,)), dec_counts, count)[0]
    enc_starts = jnp.cumsum(enc_counts) - enc_counts
    start_block = jnp.clip(enc_starts[segment] - first_block, 0, WINDOW - ENC_MOST).astype(jnp.int32)
    slice_segs = lax.dynamic_slice_in_dim(enc_segs, start_block, ENC_MOST)
    allowed_keys = jnp.repeat(slice_segs == segment, BLOCK)

    def decoder_work(operands):
        own, pieces = operands
        return attention_block(jnp.reshape(start_block, (1,)), head_gains, own, pieces, allowed_keys)

    def encoder_rest(operands):
        own, _ = operands
        zeros = jnp.zeros_like(own)
        return (zeros, (zeros,) * WINDOW, jnp.zeros((2, head_count), jnp.float32))

    produced, grads, terms = lax.cond(
        phase_index == 1, decoder_work, encoder_rest, (local_pair, window)
    )

    def added(a, b):
        return a + b

    token_total = tok_dev * count * lax.axis_size("dp")
    summed = exchange_add(terms, "phase", 1)
    back_minus = across(grads[0], [(dec(s + 1), dec(s)) for s in lower])
    back_plus = across(grads[5], [(dec(s - 1), dec(s)) for s in upper])
    own_sum = across(grads[2], [(dec(s), s) for s in range(count)])
    summed = exchange_add(exchange_add(exchange_add(summed, "dp", 1), "dp", 2), "dp", 4)
    summed, back_minus, back_plus = lax.optimization_barrier((summed, back_minus, back_plus))
    minus_sum = across(added(back_minus, grads[1]), [(dec(s + 1), s) for s in lower])
    back_plus = across(added(back_plus, grads[4]), [(dec(s - 1), dec(s)) for s in upper])
    summed = exchange_add(summed, "seq", RING)
    summed, back_plus = lax.optimization_barrier((summed, back_plus))
    plus_sum = across(added(back_plus, grads[3]), [(dec(s - 1), s) for s in upper])
    summed = ring_total(summed, shard_index)
    returned = (
        own_sum.astype(jnp.float32) + minus_sum.astype(jnp.float32) + plus_sum.astype(jnp.float32)
    ).astype(jnp.bfloat16)
    chosen = lax.dynamic_index_in_dim(summed, phase_index, 0, keepdims=False)
    scale = jnp.where(phase_index == 0, head_gains[1], 1.0) * math.sqrt(token_total)
    gain_total = chosen / scale
    result = jnp.where(phase_index == 0, returned, produced)[None]
    return (result, gain_total[None])


def solution(mesh):
    return jax.shard_map(
        local_body,
        mesh=mesh,
        in_specs=(P("phase", None, ("dp", "seq"), None), P(), P("dp", None, None)),
        out_specs=(P("phase", None, ("dp", "seq"), None), P("phase", None)),
        check_vma=False,
    )
```

```python
import math

import jax
import jax.numpy as jnp
from jax import lax
from jax.experimental import pallas as pl
from jax.experimental.pallas import tpu as pltpu
from jax.sharding import PartitionSpec as P


BLOCK = 128
ENC_MOST = 4
REACH_LOW = 2
REACH_HIGH = 3
WINDOW = REACH_LOW + REACH_HIGH + 1
RING = 8
CHUNKS = 2

masked_score = -1e30


def attention_kernel(start_ref, gains_ref, own_ref, *refs):
    window_refs = refs[:WINDOW]
    allow_ref = refs[WINDOW]
    out_ref = refs[WINDOW + 1]
    grad_refs = refs[WINDOW + 2 : 2 * WINDOW + 2]
    gain_ref = refs[2 * WINDOW + 2]
    pair = pl.program_id(0)
    start = start_ref[0]
    width = own_ref.shape[2]
    half = width // 2
    inv_root = 1.0 / math.sqrt(half)
    q = own_ref[0]
    do = own_ref[1]
    blocks = [ref[...] for ref in window_refs]

    def pick(slot):
        chosen = blocks[slot + WINDOW - ENC_MOST]
        for shift in range(WINDOW - ENC_MOST - 1, -1, -1):
            chosen = jnp.where(start == shift, blocks[slot + shift], chosen)
        return chosen

    slots = [pick(slot) for slot in range(ENC_MOST)]
    k = jnp.concatenate([piece[0] for piece in slots], axis=0)
    v = jnp.concatenate([piece[1] for piece in slots], axis=0)
    allowed = allow_ref[...] > 0
    lane = lax.broadcasted_iota(jnp.int32, (1, width), 1)
    first = lane < half
    heads = []
    att_parts = []
    for j in range(2):
        head = pair * 2 + j
        g_logit = gains_ref[0, head]
        g_value = gains_ref[1, head]
        mine = first if j == 0 else jnp.logical_not(first)
        q_h = jnp.where(mine, q, jnp.zeros_like(q))
        raw = lax.dot_general(q_h, k, (((1,), (1,)), ((), ())), preferred_element_type=jnp.float32)
        logits = jnp.where(allowed, (g_logit * inv_root) * raw, masked_score)
        top = jnp.max(logits, axis=1, keepdims=True)
        lifted = jnp.exp(logits - top)
        chances = lifted * (1.0 / jnp.sum(lifted, axis=1, keepdims=True))
        p_low = chances.astype(jnp.bfloat16)
        att_parts.append(jnp.dot(p_low, v, preferred_element_type=jnp.float32) * g_value)
        heads.append((g_logit, g_value, mine, raw, chances, p_low))
    attended = jnp.where(first, att_parts[0], att_parts[1]).astype(jnp.bfloat16)
    out_ref[0] = attended
    prod = do.astype(jnp.float32) * attended.astype(jnp.float32)
    dq_parts, dk_parts, dv_parts, logit_terms = [], [], [], []
    for g_logit, g_value, mine, raw, chances, p_low in heads:
        do_h = jnp.where(mine, do, jnp.zeros_like(do))
        slope = lax.dot_general(do_h, v, (((1,), (1,)), ((), ())), preferred_element_type=jnp.float32) * g_value
        carried = jnp.sum(jnp.where(mine, prod, 0.0), axis=1, keepdims=True)
        score_grad = chances * (slope - carried)
        score_low = score_grad.astype(jnp.bfloat16)
        factor = g_logit * inv_root
        dq_parts.append(jnp.dot(score_low, k, preferred_element_type=jnp.float32) * factor)
        dk_parts.append(lax.dot_general(score_low, q, (((0,), (0,)), ((), ())), preferred_element_type=jnp.float32) * factor)
        dv_parts.append(lax.dot_general(p_low, do, (((0,), (0,)), ((), ())), preferred_element_type=jnp.float32) * g_value)
        logit_terms.append(jnp.sum(score_grad * raw) * inv_root)
    out_ref[1] = jnp.where(first, dq_parts[0], dq_parts[1]).astype(jnp.bfloat16)
    key_grad = jnp.where(first, dk_parts[0], dk_parts[1]).astype(jnp.bfloat16)
    value_grad = jnp.where(first, dv_parts[0], dv_parts[1]).astype(jnp.bfloat16)
    value_prod = v.astype(jnp.float32) * value_grad.astype(jnp.float32)
    value_terms = [jnp.sum(jnp.where(first, value_prod, 0.0)), jnp.sum(jnp.where(first, 0.0, value_prod))]
    zero_block = jnp.zeros((BLOCK, width), jnp.bfloat16)
    for position in range(WINDOW):
        key_block = zero_block
        value_block = zero_block
        for slot in range(ENC_MOST):
            if 0 <= position - slot <= WINDOW - ENC_MOST:
                rows = slice(slot * BLOCK, (slot + 1) * BLOCK)
                key_block = jnp.where(start == position - slot, key_grad[rows], key_block)
                value_block = jnp.where(start == position - slot, value_grad[rows], value_block)
        grad_refs[position][0] = key_block
        grad_refs[position][1] = value_block
    glane = lax.broadcasted_iota(jnp.int32, gain_ref.shape, 2)
    terms = value_terms + logit_terms
    packed = jnp.zeros(gain_ref.shape, jnp.float32)
    for index, term in enumerate(terms):
        packed = jnp.where(glane == index, term, packed)
    gain_ref[...] = packed


def attention_block(start, head_gains, own, window, allowed_keys):
    _, rows, inner = own.shape
    keys = ENC_MOST * BLOCK
    head_count = head_gains.shape[1]
    width = 2 * (inner // head_count)
    pairs = inner // width
    block_spec = pl.BlockSpec((2, rows, width), lambda i, s, g: (0, 0, i))
    grid_spec = pltpu.PrefetchScalarGridSpec(
        num_scalar_prefetch=2,
        grid=(pairs,),
        in_specs=[block_spec] * (WINDOW + 1) + [pl.BlockSpec((1, keys), lambda i, s, g: (0, 0))],
        out_specs=[block_spec] * (WINDOW + 1) + [pl.BlockSpec((1, 8, 128), lambda i, s, g: (i, 0, 0))],
    )
    flops = 2 * rows * keys * width * 6 * pairs * 2
    cost = pl.CostEstimate(
        flops=flops,
        transcendentals=rows * keys * head_count,
        bytes_accessed=2 * 2 * rows * inner * (2 * WINDOW + 2),
    )
    outs = pl.pallas_call(
        attention_kernel,
        grid_spec=grid_spec,
        out_shape=[jax.ShapeDtypeStruct(own.shape, jnp.bfloat16)] * (WINDOW + 1)
        + [jax.ShapeDtypeStruct((pairs, 8, 128), jnp.float32)],
        cost_estimate=cost,
    )(start, head_gains, own, *window, allowed_keys.astype(jnp.int32)[None, :])
    produced = outs[0]
    grads = tuple(outs[1 : WINDOW + 1])
    packed = outs[WINDOW + 1]
    terms = jnp.stack([packed[:, 0, 0:2].reshape(-1), packed[:, 0, 2:4].reshape(-1)])
    return produced, grads, terms


def ring_shift(value, steps):
    count = lax.axis_size("seq")
    pairs = []
    for source in range(count):
        base = source - source % RING
        pairs.append((source, base + (source - steps) % RING))
    return lax.ppermute(value, "seq", pairs)


def ring_total(value, shard_index):
    gathered = value[None]
    gathered = jnp.concatenate([gathered, ring_shift(gathered, 1)], axis=0)
    gathered = jnp.concatenate([gathered, ring_shift(gathered, 2)], axis=0)
    while gathered.shape[0] < RING:
        have = gathered.shape[0]
        gathered = jnp.concatenate([gathered, ring_shift(gathered, 2)[have - 2 : have]], axis=0)
    ordered = jnp.roll(gathered, shard_index % RING, axis=0)
    total = ordered[0]
    for index in range(1, RING):
        total = total + ordered[index]
    return total


def exchange_add(value, axis, stride):
    count = lax.axis_size(axis)
    return value + lax.ppermute(value, axis, [(i, i ^ stride) for i in range(count)])


def segment_of(block_ids, block_sizes, block_total):
    starts = jnp.cumsum(block_sizes) - block_sizes
    found = jnp.sum((starts[None, :] <= block_ids[:, None]).astype(jnp.int32), axis=1) - 1
    inside = jnp.logical_and(block_ids >= 0, block_ids < block_total)
    return jnp.where(inside, found, -1)


def local_body(sections, head_gains, block_counts):
    phase_index = lax.axis_index("phase")
    shard_index = lax.axis_index("seq")
    count = lax.axis_size("seq")
    local_pair = sections[0]
    tok_dev = local_pair.shape[1]
    inner = local_pair.shape[2]
    head_count = head_gains.shape[1]
    enc_counts = block_counts[0, 0]
    dec_counts = block_counts[0, 1]

    def dec(s):
        return count + s

    def across(value, pairs):
        return lax.ppermute(value, ("phase", "seq"), pairs)

    lower = range(count - 1)
    upper = range(1, count)

    def forward(pair):
        at_home = across(pair, [(s, dec(s)) for s in range(count)])
        minus_1 = across(pair, [(s + 1, dec(s)) for s in lower])
        plus_1 = across(pair, [(s - 1, dec(s)) for s in upper])
        minus_2 = across(minus_1, [(dec(s + 1), dec(s)) for s in lower])
        plus_2 = across(plus_1, [(dec(s - 1), dec(s)) for s in upper])
        minus_3 = across(minus_2, [(dec(s + 1), dec(s)) for s in lower])
        return [plus_2, plus_1, at_home, minus_1, minus_2, minus_3]

    first_block = shard_index - REACH_LOW
    window_blocks = first_block + jnp.arange(WINDOW, dtype=jnp.int32)
    enc_segs = segment_of(window_blocks, enc_counts, count)
    segment = segment_of(jnp.reshape(shard_index, (1,)), dec_counts, count)[0]
    enc_starts = jnp.cumsum(enc_counts) - enc_counts
    start_block = jnp.clip(enc_starts[segment] - first_block, 0, WINDOW - ENC_MOST).astype(jnp.int32)
    slice_segs = lax.dynamic_slice_in_dim(enc_segs, start_block, ENC_MOST)
    allowed_keys = jnp.repeat(slice_segs == segment, BLOCK)
    start = jnp.reshape(start_block, (1,))

    width = inner // CHUNKS
    heads = head_count // CHUNKS
    pairs = [local_pair[:, :, c * width : (c + 1) * width] for c in range(CHUNKS)]
    gains = [head_gains[:, c * heads : (c + 1) * heads] for c in range(CHUNKS)]
    windows = []
    for c in range(CHUNKS):
        windows.append(forward(pairs[c]))
    outs = []
    for c in range(CHUNKS):
        outs.append(attention_block(start, gains[c], pairs[c], windows[c], allowed_keys))

    def backward(grads):
        back_minus = across(grads[0], [(dec(s + 1), dec(s)) for s in lower])
        back_plus = across(grads[5], [(dec(s - 1), dec(s)) for s in upper])
        own_sum = across(grads[2], [(dec(s), s) for s in range(count)])
        minus_sum = across(back_minus + grads[1], [(dec(s + 1), s) for s in lower])
        back_plus = across(back_plus + grads[4], [(dec(s - 1), dec(s)) for s in upper])
        plus_sum = across(back_plus + grads[3], [(dec(s - 1), s) for s in upper])
        return own_sum, minus_sum, plus_sum

    terms = jnp.concatenate([out[2] for out in outs], axis=1)
    terms = jnp.where(phase_index == 1, terms, 0.0)
    returned_parts = []
    for c in range(CHUNKS - 1):
        returned_parts.append(backward(outs[c][1]))

    grads = outs[CHUNKS - 1][1]
    token_total = tok_dev * count * lax.axis_size("dp")
    summed = exchange_add(terms, "phase", 1)
    back_minus = across(grads[0], [(dec(s + 1), dec(s)) for s in lower])
    back_plus = across(grads[5], [(dec(s - 1), dec(s)) for s in upper])
    own_sum = across(grads[2], [(dec(s), s) for s in range(count)])
    summed = exchange_add(exchange_add(exchange_add(summed, "dp", 1), "dp", 2), "dp", 4)
    summed, back_minus, back_plus = lax.optimization_barrier((summed, back_minus, back_plus))
    minus_sum = across(back_minus + grads[1], [(dec(s + 1), s) for s in lower])
    back_plus = across(back_plus + grads[4], [(dec(s - 1), dec(s)) for s in upper])
    summed = exchange_add(summed, "seq", RING)
    summed, back_plus = lax.optimization_barrier((summed, back_plus))
    plus_sum = across(back_plus + grads[3], [(dec(s - 1), s) for s in upper])
    summed = ring_total(summed, shard_index)
    returned_parts.append((own_sum, minus_sum, plus_sum))

    returned = jnp.concatenate(
        [
            (a.astype(jnp.float32) + b.astype(jnp.float32) + d.astype(jnp.float32)).astype(jnp.bfloat16)
            for a, b, d in returned_parts
        ],
        axis=2,
    )
    produced = jnp.concatenate([out[0] for out in outs], axis=2)
    chosen = lax.dynamic_index_in_dim(summed, phase_index, 0, keepdims=False)
    scale = jnp.where(phase_index == 0, head_gains[1], 1.0) * math.sqrt(token_total)
    gain_total = chosen / scale
    result = jnp.where(phase_index == 0, returned, produced)[None]
    return (result, gain_total[None])


def solution(mesh):
    return jax.shard_map(
        local_body,
        mesh=mesh,
        in_specs=(P("phase", None, ("dp", "seq"), None), P(), P("dp", None, None)),
        out_specs=(P("phase", None, ("dp", "seq"), None), P("phase", None)),
        check_vma=False,
    )
```

```python
import math

import jax
import jax.numpy as jnp
from jax import lax
from jax.experimental import pallas as pl
from jax.experimental.pallas import tpu as pltpu
from jax.sharding import PartitionSpec as P


BLOCK = 128
ENC_MOST = 4
REACH_LOW = 2
REACH_HIGH = 3
WINDOW = REACH_LOW + REACH_HIGH + 1
RING = 8

masked_score = -1e30


def attention_kernel(start_ref, gains_ref, own_ref, *refs):
    window_refs = refs[:WINDOW]
    allow_ref = refs[WINDOW]
    out_ref = refs[WINDOW + 1]
    grad_refs = refs[WINDOW + 2 : 2 * WINDOW + 2]
    gain_ref = refs[2 * WINDOW + 2]
    pair = pl.program_id(0)
    start = start_ref[0]
    width = own_ref.shape[2]
    half = width // 2
    inv_root = 1.0 / math.sqrt(half)
    q = own_ref[0]
    do = own_ref[1]
    blocks = [ref[...] for ref in window_refs]

    def pick(slot):
        chosen = blocks[slot + WINDOW - ENC_MOST]
        for shift in range(WINDOW - ENC_MOST - 1, -1, -1):
            chosen = jnp.where(start == shift, blocks[slot + shift], chosen)
        return chosen

    slots = [pick(slot) for slot in range(ENC_MOST)]
    k = jnp.concatenate([piece[0] for piece in slots], axis=0)
    v = jnp.concatenate([piece[1] for piece in slots], axis=0)
    allowed = allow_ref[...] > 0
    lane = lax.broadcasted_iota(jnp.int32, (1, width), 1)
    first = lane < half
    heads = []
    att_parts = []
    for j in range(2):
        head = pair * 2 + j
        g_logit = gains_ref[0, head]
        g_value = gains_ref[1, head]
        mine = first if j == 0 else jnp.logical_not(first)
        q_h = jnp.where(mine, q, jnp.zeros_like(q))
        raw = lax.dot_general(q_h, k, (((1,), (1,)), ((), ())), preferred_element_type=jnp.float32)
        logits = jnp.where(allowed, (g_logit * inv_root) * raw, masked_score)
        top = jnp.max(logits, axis=1, keepdims=True)
        lifted = jnp.exp(logits - top)
        chances = lifted * (1.0 / jnp.sum(lifted, axis=1, keepdims=True))
        p_low = chances.astype(jnp.bfloat16)
        att_parts.append(jnp.dot(p_low, v, preferred_element_type=jnp.float32) * g_value)
        heads.append((g_logit, g_value, mine, raw, chances, p_low))
    attended = jnp.where(first, att_parts[0], att_parts[1]).astype(jnp.bfloat16)
    out_ref[0] = attended
    prod = do.astype(jnp.float32) * attended.astype(jnp.float32)
    dq_parts, dk_parts, dv_parts, logit_terms = [], [], [], []
    for g_logit, g_value, mine, raw, chances, p_low in heads:
        do_h = jnp.where(mine, do, jnp.zeros_like(do))
        slope = lax.dot_general(do_h, v, (((1,), (1,)), ((), ())), preferred_element_type=jnp.float32) * g_value
        carried = jnp.sum(jnp.where(mine, prod, 0.0), axis=1, keepdims=True)
        score_grad = chances * (slope - carried)
        score_low = score_grad.astype(jnp.bfloat16)
        factor = g_logit * inv_root
        dq_parts.append(jnp.dot(score_low, k, preferred_element_type=jnp.float32) * factor)
        dk_parts.append(lax.dot_general(score_low, q, (((0,), (0,)), ((), ())), preferred_element_type=jnp.float32) * factor)
        dv_parts.append(lax.dot_general(p_low, do, (((0,), (0,)), ((), ())), preferred_element_type=jnp.float32) * g_value)
        logit_terms.append(jnp.sum(score_grad * raw) * inv_root)
    out_ref[1] = jnp.where(first, dq_parts[0], dq_parts[1]).astype(jnp.bfloat16)
    key_grad = jnp.where(first, dk_parts[0], dk_parts[1]).astype(jnp.bfloat16)
    value_grad = jnp.where(first, dv_parts[0], dv_parts[1]).astype(jnp.bfloat16)
    value_prod = v.astype(jnp.float32) * value_grad.astype(jnp.float32)
    value_terms = [jnp.sum(jnp.where(first, value_prod, 0.0)), jnp.sum(jnp.where(first, 0.0, value_prod))]
    zero_block = jnp.zeros((BLOCK, width), jnp.bfloat16)
    for position in range(WINDOW):
        key_block = zero_block
        value_block = zero_block
        for slot in range(ENC_MOST):
            if 0 <= position - slot <= WINDOW - ENC_MOST:
                rows = slice(slot * BLOCK, (slot + 1) * BLOCK)
                key_block = jnp.where(start == position - slot, key_grad[rows], key_block)
                value_block = jnp.where(start == position - slot, value_grad[rows], value_block)
        grad_refs[position][0] = key_block
        grad_refs[position][1] = value_block
    glane = lax.broadcasted_iota(jnp.int32, gain_ref.shape, 2)
    terms = value_terms + logit_terms
    packed = jnp.zeros(gain_ref.shape, jnp.float32)
    for index, term in enumerate(terms):
        packed = jnp.where(glane == index, term, packed)
    gain_ref[...] = packed


def attention_block(start, head_gains, own, window, allowed_keys):
    _, rows, inner = own.shape
    keys = ENC_MOST * BLOCK
    head_count = head_gains.shape[1]
    width = 2 * (inner // head_count)
    pairs = inner // width
    block_spec = pl.BlockSpec((2, rows, width), lambda i, s, g: (0, 0, i))
    grid_spec = pltpu.PrefetchScalarGridSpec(
        num_scalar_prefetch=2,
        grid=(pairs,),
        in_specs=[block_spec] * (WINDOW + 1) + [pl.BlockSpec((1, keys), lambda i, s, g: (0, 0))],
        out_specs=[block_spec] * (WINDOW + 1) + [pl.BlockSpec((1, 8, 128), lambda i, s, g: (i, 0, 0))],
    )
    flops = 2 * rows * keys * width * 6 * pairs * 2
    cost = pl.CostEstimate(
        flops=flops,
        transcendentals=rows * keys * head_count,
        bytes_accessed=2 * 2 * rows * inner * (2 * WINDOW + 2),
    )
    outs = pl.pallas_call(
        attention_kernel,
        grid_spec=grid_spec,
        out_shape=[jax.ShapeDtypeStruct(own.shape, jnp.bfloat16)] * (WINDOW + 1)
        + [jax.ShapeDtypeStruct((pairs, 8, 128), jnp.float32)],
        cost_estimate=cost,
    )(start, head_gains, own, *window, allowed_keys.astype(jnp.int32)[None, :])
    produced = outs[0]
    grads = tuple(outs[1 : WINDOW + 1])
    packed = outs[WINDOW + 1]
    terms = jnp.stack([packed[:, 0, 0:2].reshape(-1), packed[:, 0, 2:4].reshape(-1)])
    return produced, grads, terms


def ring_shift(value, steps):
    count = lax.axis_size("seq")
    pairs = []
    for source in range(count):
        base = source - source % RING
        pairs.append((source, base + (source - steps) % RING))
    return lax.ppermute(value, ("phase", "seq"), pairs)


def ring_total(value, shard_index):
    gathered = value[None]
    gathered = jnp.concatenate([gathered, ring_shift(gathered, 1)], axis=0)
    gathered = jnp.concatenate([gathered, ring_shift(gathered, 2)], axis=0)
    while gathered.shape[0] < RING:
        have = gathered.shape[0]
        gathered = jnp.concatenate([gathered, ring_shift(gathered, 2)[have - 2 : have]], axis=0)
    ordered = jnp.roll(gathered, shard_index % RING, axis=0)
    total = ordered[0]
    for index in range(1, RING):
        total = total + ordered[index]
    return total


def exchange_add(value, axis, stride):
    count = lax.axis_size(axis)
    return value + lax.ppermute(value, ("phase", axis), [(i, i ^ stride) for i in range(count)])


def segment_of(block_ids, block_sizes, block_total):
    starts = jnp.cumsum(block_sizes) - block_sizes
    found = jnp.sum((starts[None, :] <= block_ids[:, None]).astype(jnp.int32), axis=1) - 1
    inside = jnp.logical_and(block_ids >= 0, block_ids < block_total)
    return jnp.where(inside, found, -1)


def local_body(sections, head_gains, block_counts):
    phase_index = lax.axis_index("phase")
    shard_index = lax.axis_index("seq")
    count = lax.axis_size("seq")
    local_pair = sections[0]
    tok_dev = local_pair.shape[1]
    head_count = head_gains.shape[1]
    enc_counts = block_counts[0, 0]
    dec_counts = block_counts[0, 1]

    def dec(s):
        return count + s

    def across(value, pairs):
        return lax.ppermute(value, ("phase", "seq"), pairs)

    lower = range(count - 1)
    upper = range(1, count)
    at_home = across(local_pair, [(s, dec(s)) for s in range(count)])
    minus_1 = across(local_pair, [(s + 1, dec(s)) for s in lower])
    plus_1 = across(local_pair, [(s - 1, dec(s)) for s in upper])
    minus_2 = across(minus_1, [(dec(s + 1), dec(s)) for s in lower])
    plus_2 = across(plus_1, [(dec(s - 1), dec(s)) for s in upper])
    minus_3 = across(minus_2, [(dec(s + 1), dec(s)) for s in lower])
    window = [plus_2, plus_1, at_home, minus_1, minus_2, minus_3]

    first_block = shard_index - REACH_LOW
    window_blocks = first_block + jnp.arange(WINDOW, dtype=jnp.int32)
    enc_segs = segment_of(window_blocks, enc_counts, count)
    segment = segment_of(jnp.reshape(shard_index, (1,)), dec_counts, count)[0]
    enc_starts = jnp.cumsum(enc_counts) - enc_counts
    start_block = jnp.clip(enc_starts[segment] - first_block, 0, WINDOW - ENC_MOST).astype(jnp.int32)
    slice_segs = lax.dynamic_slice_in_dim(enc_segs, start_block, ENC_MOST)
    allowed_keys = jnp.repeat(slice_segs == segment, BLOCK)

    def decoder_work(operands):
        own, pieces = operands
        return attention_block(jnp.reshape(start_block, (1,)), head_gains, own, pieces, allowed_keys)

    def encoder_rest(operands):
        own, _ = operands
        zeros = jnp.zeros_like(own)
        return (zeros, (zeros,) * WINDOW, jnp.zeros((2, head_count), jnp.float32))

    produced, grads, terms = lax.cond(
        phase_index == 1, decoder_work, encoder_rest, (local_pair, window)
    )

    def added(a, b):
        return a + b

    token_total = tok_dev * count * lax.axis_size("dp")
    summed = lax.ppermute(terms, "phase", [(1, 0)])
    back_minus = across(grads[0], [(dec(s + 1), dec(s)) for s in lower])
    back_plus = across(grads[5], [(dec(s - 1), dec(s)) for s in upper])
    own_sum = across(grads[2], [(dec(s), s) for s in range(count)])
    summed = exchange_add(exchange_add(exchange_add(summed, "dp", 1), "dp", 2), "dp", 4)
    summed, back_minus, back_plus = lax.optimization_barrier((summed, back_minus, back_plus))
    minus_sum = across(added(back_minus, grads[1]), [(dec(s + 1), s) for s in lower])
    back_plus = across(added(back_plus, grads[4]), [(dec(s - 1), dec(s)) for s in upper])
    summed = exchange_add(summed, "seq", RING)
    summed, back_plus = lax.optimization_barrier((summed, back_plus))
    plus_sum = across(added(back_plus, grads[3]), [(dec(s - 1), s) for s in upper])
    summed = ring_total(summed, shard_index)
    returned = (
        own_sum.astype(jnp.float32) + minus_sum.astype(jnp.float32) + plus_sum.astype(jnp.float32)
    ).astype(jnp.bfloat16)
    shared = lax.ppermute(summed, "phase", [(0, 1)])
    chosen = jnp.where(phase_index == 0, summed[0], shared[1])
    scale = jnp.where(phase_index == 0, head_gains[1], 1.0) * math.sqrt(token_total)
    gain_total = chosen / scale
    result = jnp.where(phase_index == 0, returned, produced)[None]
    return (result, gain_total[None])


def solution(mesh):
    return jax.shard_map(
        local_body,
        mesh=mesh,
        in_specs=(P("phase", None, ("dp", "seq"), None), P(), P("dp", None, None)),
        out_specs=(P("phase", None, ("dp", "seq"), None), P("phase", None)),
        check_vma=False,
    )
```

```python
import math

import jax
import jax.numpy as jnp
from jax import lax
from jax.experimental import pallas as pl
from jax.experimental.pallas import tpu as pltpu
from jax.sharding import PartitionSpec as P


BLOCK = 128
ENC_MOST = 4
REACH_LOW = 2
REACH_HIGH = 3
WINDOW = REACH_LOW + REACH_HIGH + 1

masked_score = -1e30


def attention_kernel(start_ref, gains_ref, own_ref, *refs):
    window_refs = refs[:WINDOW]
    allow_ref = refs[WINDOW]
    out_ref = refs[WINDOW + 1]
    grad_refs = refs[WINDOW + 2 : 2 * WINDOW + 2]
    gain_ref = refs[2 * WINDOW + 2]
    pair = pl.program_id(0)
    start = start_ref[0]
    width = own_ref.shape[2]
    half = width // 2
    inv_root = 1.0 / math.sqrt(half)
    q = own_ref[0]
    do = own_ref[1]
    blocks = [ref[...] for ref in window_refs]

    def pick(slot):
        chosen = blocks[slot + WINDOW - ENC_MOST]
        for shift in range(WINDOW - ENC_MOST - 1, -1, -1):
            chosen = jnp.where(start == shift, blocks[slot + shift], chosen)
        return chosen

    slots = [pick(slot) for slot in range(ENC_MOST)]
    k = jnp.concatenate([piece[0] for piece in slots], axis=0)
    v = jnp.concatenate([piece[1] for piece in slots], axis=0)
    allowed = allow_ref[...] > 0
    lane = lax.broadcasted_iota(jnp.int32, (1, width), 1)
    first = lane < half
    heads = []
    att_parts = []
    for j in range(2):
        head = pair * 2 + j
        g_logit = gains_ref[0, head]
        g_value = gains_ref[1, head]
        mine = first if j == 0 else jnp.logical_not(first)
        q_h = jnp.where(mine, q, jnp.zeros_like(q))
        raw = lax.dot_general(q_h, k, (((1,), (1,)), ((), ())), preferred_element_type=jnp.float32)
        logits = jnp.where(allowed, (g_logit * inv_root) * raw, masked_score)
        top = jnp.max(logits, axis=1, keepdims=True)
        lifted = jnp.exp(logits - top)
        chances = lifted * (1.0 / jnp.sum(lifted, axis=1, keepdims=True))
        p_low = chances.astype(jnp.bfloat16)
        att_parts.append(jnp.dot(p_low, v, preferred_element_type=jnp.float32) * g_value)
        heads.append((g_logit, g_value, mine, raw, chances, p_low))
    attended = jnp.where(first, att_parts[0], att_parts[1]).astype(jnp.bfloat16)
    out_ref[0] = attended
    prod = do.astype(jnp.float32) * attended.astype(jnp.float32)
    dq_parts, dk_parts, dv_parts, logit_terms = [], [], [], []
    for g_logit, g_value, mine, raw, chances, p_low in heads:
        do_h = jnp.where(mine, do, jnp.zeros_like(do))
        slope = lax.dot_general(do_h, v, (((1,), (1,)), ((), ())), preferred_element_type=jnp.float32) * g_value
        carried = jnp.sum(jnp.where(mine, prod, 0.0), axis=1, keepdims=True)
        score_grad = chances * (slope - carried)
        score_low = score_grad.astype(jnp.bfloat16)
        factor = g_logit * inv_root
        dq_parts.append(jnp.dot(score_low, k, preferred_element_type=jnp.float32) * factor)
        dk_parts.append(lax.dot_general(score_low, q, (((0,), (0,)), ((), ())), preferred_element_type=jnp.float32) * factor)
        dv_parts.append(lax.dot_general(p_low, do, (((0,), (0,)), ((), ())), preferred_element_type=jnp.float32) * g_value)
        logit_terms.append(jnp.sum(score_grad * raw) * inv_root)
    out_ref[1] = jnp.where(first, dq_parts[0], dq_parts[1]).astype(jnp.bfloat16)
    key_grad = jnp.where(first, dk_parts[0], dk_parts[1]).astype(jnp.bfloat16)
    value_grad = jnp.where(first, dv_parts[0], dv_parts[1]).astype(jnp.bfloat16)
    value_prod = v.astype(jnp.float32) * value_grad.astype(jnp.float32)
    value_terms = [jnp.sum(jnp.where(first, value_prod, 0.0)), jnp.sum(jnp.where(first, 0.0, value_prod))]
    zero_block = jnp.zeros((BLOCK, width), jnp.bfloat16)
    for position in range(WINDOW):
        key_block = zero_block
        value_block = zero_block
        for slot in range(ENC_MOST):
            if 0 <= position - slot <= WINDOW - ENC_MOST:
                rows = slice(slot * BLOCK, (slot + 1) * BLOCK)
                key_block = jnp.where(start == position - slot, key_grad[rows], key_block)
                value_block = jnp.where(start == position - slot, value_grad[rows], value_block)
        grad_refs[position][0] = key_block
        grad_refs[position][1] = value_block
    glane = lax.broadcasted_iota(jnp.int32, gain_ref.shape, 2)
    terms = value_terms + logit_terms
    packed = jnp.zeros(gain_ref.shape, jnp.float32)
    for index, term in enumerate(terms):
        packed = jnp.where(glane == index, term, packed)
    gain_ref[...] = packed


def attention_block(start, head_gains, own, window, allowed_keys):
    _, rows, inner = own.shape
    keys = ENC_MOST * BLOCK
    head_count = head_gains.shape[1]
    width = 2 * (inner // head_count)
    pairs = inner // width
    block_spec = pl.BlockSpec((2, rows, width), lambda i, s, g: (0, 0, i))
    grid_spec = pltpu.PrefetchScalarGridSpec(
        num_scalar_prefetch=2,
        grid=(pairs,),
        in_specs=[block_spec] * (WINDOW + 1) + [pl.BlockSpec((1, keys), lambda i, s, g: (0, 0))],
        out_specs=[block_spec] * (WINDOW + 1) + [pl.BlockSpec((1, 8, 128), lambda i, s, g: (i, 0, 0))],
    )
    flops = 2 * rows * keys * width * 6 * pairs * 2
    cost = pl.CostEstimate(
        flops=flops,
        transcendentals=rows * keys * head_count,
        bytes_accessed=2 * 2 * rows * inner * (2 * WINDOW + 2),
    )
    outs = pl.pallas_call(
        attention_kernel,
        grid_spec=grid_spec,
        out_shape=[jax.ShapeDtypeStruct(own.shape, jnp.bfloat16)] * (WINDOW + 1)
        + [jax.ShapeDtypeStruct((pairs, 8, 128), jnp.float32)],
        cost_estimate=cost,
    )(start, head_gains, own, *window, allowed_keys.astype(jnp.int32)[None, :])
    produced = outs[0]
    grads = tuple(outs[1 : WINDOW + 1])
    packed = outs[WINDOW + 1]
    terms = jnp.stack([packed[:, 0, 0:2].reshape(-1), packed[:, 0, 2:4].reshape(-1)])
    return produced, grads, terms


def group_total(value, axis, size, stride, index):
    count = lax.axis_size(axis)
    gathered = [value]
    for shift in range(1, size):
        pairs = []
        for source in range(count):
            position = (source // stride) % size
            base = source - position * stride
            pairs.append((source, base + ((position - shift) % size) * stride))
        gathered.append(lax.ppermute(value, ("phase", axis), pairs))
    ordered = jnp.roll(jnp.stack(gathered), (index // stride) % size, axis=0)
    total = ordered[0]
    for position in range(1, size):
        total = total + ordered[position]
    return total


def segment_of(block_ids, block_sizes, block_total):
    starts = jnp.cumsum(block_sizes) - block_sizes
    found = jnp.sum((starts[None, :] <= block_ids[:, None]).astype(jnp.int32), axis=1) - 1
    inside = jnp.logical_and(block_ids >= 0, block_ids < block_total)
    return jnp.where(inside, found, -1)


def local_body(sections, head_gains, block_counts):
    phase_index = lax.axis_index("phase")
    shard_index = lax.axis_index("seq")
    count = lax.axis_size("seq")
    local_pair = sections[0]
    tok_dev = local_pair.shape[1]
    head_count = head_gains.shape[1]
    enc_counts = block_counts[0, 0]
    dec_counts = block_counts[0, 1]

    def dec(s):
        return count + s

    def across(value, pairs):
        return lax.ppermute(value, ("phase", "seq"), pairs)

    lower = range(count - 1)
    upper = range(1, count)
    at_home = across(local_pair, [(s, dec(s)) for s in range(count)])
    minus_1 = across(local_pair, [(s + 1, dec(s)) for s in lower])
    plus_1 = across(local_pair, [(s - 1, dec(s)) for s in upper])
    minus_2 = across(minus_1, [(dec(s + 1), dec(s)) for s in lower])
    plus_2 = across(plus_1, [(dec(s - 1), dec(s)) for s in upper])
    minus_3 = across(minus_2, [(dec(s + 1), dec(s)) for s in lower])
    window = [plus_2, plus_1, at_home, minus_1, minus_2, minus_3]

    first_block = shard_index - REACH_LOW
    window_blocks = first_block + jnp.arange(WINDOW, dtype=jnp.int32)
    enc_segs = segment_of(window_blocks, enc_counts, count)
    segment = segment_of(jnp.reshape(shard_index, (1,)), dec_counts, count)[0]
    enc_starts = jnp.cumsum(enc_counts) - enc_counts
    start_block = jnp.clip(enc_starts[segment] - first_block, 0, WINDOW - ENC_MOST).astype(jnp.int32)
    slice_segs = lax.dynamic_slice_in_dim(enc_segs, start_block, ENC_MOST)
    allowed_keys = jnp.repeat(slice_segs == segment, BLOCK)

    def decoder_work(operands):
        own, pieces = operands
        return attention_block(jnp.reshape(start_block, (1,)), head_gains, own, pieces, allowed_keys)

    def encoder_rest(operands):
        own, _ = operands
        zeros = jnp.zeros_like(own)
        return (zeros, (zeros,) * WINDOW, jnp.zeros((2, head_count), jnp.float32))

    produced, grads, terms = lax.cond(
        phase_index == 1, decoder_work, encoder_rest, (local_pair, window)
    )

    def added(a, b):
        return a + b

    token_total = tok_dev * count * lax.axis_size("dp")
    dp_index = lax.axis_index("dp")
    summed = lax.ppermute(terms, "phase", [(1, 0)])
    back_minus = across(grads[0], [(dec(s + 1), dec(s)) for s in lower])
    back_plus = across(grads[5], [(dec(s - 1), dec(s)) for s in upper])
    own_sum = across(grads[2], [(dec(s), s) for s in range(count)])
    summed = group_total(summed, "dp", 4, 1, dp_index)
    summed = group_total(summed, "dp", 2, 4, dp_index)
    summed, back_minus, back_plus = lax.optimization_barrier((summed, back_minus, back_plus))
    minus_sum = across(added(back_minus, grads[1]), [(dec(s + 1), s) for s in lower])
    back_plus = across(added(back_plus, grads[4]), [(dec(s - 1), dec(s)) for s in upper])
    summed = group_total(summed, "seq", 4, 1, shard_index)
    summed, back_plus = lax.optimization_barrier((summed, back_plus))
    plus_sum = across(added(back_plus, grads[3]), [(dec(s - 1), s) for s in upper])
    summed = group_total(summed, "seq", 4, 4, shard_index)
    returned = (
        own_sum.astype(jnp.float32) + minus_sum.astype(jnp.float32) + plus_sum.astype(jnp.float32)
    ).astype(jnp.bfloat16)
    shared = lax.ppermute(summed, "phase", [(0, 1)])
    chosen = jnp.where(phase_index == 0, summed[0], shared[1])
    scale = jnp.where(phase_index == 0, head_gains[1], 1.0) * math.sqrt(token_total)
    gain_total = chosen / scale
    result = jnp.where(phase_index == 0, returned, produced)[None]
    return (result, gain_total[None])


def solution(mesh):
    return jax.shard_map(
        local_body,
        mesh=mesh,
        in_specs=(P("phase", None, ("dp", "seq"), None), P(), P("dp", None, None)),
        out_specs=(P("phase", None, ("dp", "seq"), None), P("phase", None)),
        check_vma=False,
    )
```

```python
import math

import jax
import jax.numpy as jnp
from jax import lax
from jax.experimental import pallas as pl
from jax.experimental.pallas import tpu as pltpu
from jax.sharding import PartitionSpec as P


BLOCK = 128
ENC_MOST = 4
REACH_LOW = 2
REACH_HIGH = 3
WINDOW = REACH_LOW + REACH_HIGH + 1
RING = 8

masked_score = -1e30


def attention_kernel(start_ref, gains_ref, own_ref, *refs):
    window_refs = refs[:WINDOW]
    allow_ref = refs[WINDOW]
    out_ref = refs[WINDOW + 1]
    grad_refs = refs[WINDOW + 2 : 2 * WINDOW + 2]
    gain_ref = refs[2 * WINDOW + 2]
    pair = pl.program_id(0)
    start = start_ref[0]
    width = own_ref.shape[2]
    half = width // 2
    inv_root = 1.0 / math.sqrt(half)
    q = own_ref[0]
    do = own_ref[1]
    blocks = [ref[...] for ref in window_refs]

    def pick(slot):
        chosen = blocks[slot + WINDOW - ENC_MOST]
        for shift in range(WINDOW - ENC_MOST - 1, -1, -1):
            chosen = jnp.where(start == shift, blocks[slot + shift], chosen)
        return chosen

    slots = [pick(slot) for slot in range(ENC_MOST)]
    k = jnp.concatenate([piece[0] for piece in slots], axis=0)
    v = jnp.concatenate([piece[1] for piece in slots], axis=0)
    allowed = allow_ref[...] > 0
    lane = lax.broadcasted_iota(jnp.int32, (1, width), 1)
    first = lane < half
    heads = []
    att_parts = []
    for j in range(2):
        head = pair * 2 + j
        g_logit = gains_ref[0, head]
        g_value = gains_ref[1, head]
        mine = first if j == 0 else jnp.logical_not(first)
        q_h = jnp.where(mine, q, jnp.zeros_like(q))
        raw = lax.dot_general(q_h, k, (((1,), (1,)), ((), ())), preferred_element_type=jnp.float32)
        logits = jnp.where(allowed, (g_logit * inv_root) * raw, masked_score)
        top = jnp.max(logits, axis=1, keepdims=True)
        lifted = jnp.exp(logits - top)
        chances = lifted * (1.0 / jnp.sum(lifted, axis=1, keepdims=True))
        p_low = chances.astype(jnp.bfloat16)
        att_parts.append(jnp.dot(p_low, v, preferred_element_type=jnp.float32) * g_value)
        heads.append((g_logit, g_value, mine, raw, chances, p_low))
    attended = jnp.where(first, att_parts[0], att_parts[1]).astype(jnp.bfloat16)
    out_ref[0] = attended
    prod = do.astype(jnp.float32) * attended.astype(jnp.float32)
    dq_parts, dk_parts, dv_parts, logit_terms = [], [], [], []
    for g_logit, g_value, mine, raw, chances, p_low in heads:
        do_h = jnp.where(mine, do, jnp.zeros_like(do))
        slope = lax.dot_general(do_h, v, (((1,), (1,)), ((), ())), preferred_element_type=jnp.float32) * g_value
        carried = jnp.sum(jnp.where(mine, prod, 0.0), axis=1, keepdims=True)
        score_grad = chances * (slope - carried)
        score_low = score_grad.astype(jnp.bfloat16)
        factor = g_logit * inv_root
        dq_parts.append(jnp.dot(score_low, k, preferred_element_type=jnp.float32) * factor)
        dk_parts.append(lax.dot_general(score_low, q, (((0,), (0,)), ((), ())), preferred_element_type=jnp.float32) * factor)
        dv_parts.append(lax.dot_general(p_low, do, (((0,), (0,)), ((), ())), preferred_element_type=jnp.float32) * g_value)
        logit_terms.append(jnp.sum(score_grad * raw) * inv_root)
    out_ref[1] = jnp.where(first, dq_parts[0], dq_parts[1]).astype(jnp.bfloat16)
    key_grad = jnp.where(first, dk_parts[0], dk_parts[1]).astype(jnp.bfloat16)
    value_grad = jnp.where(first, dv_parts[0], dv_parts[1]).astype(jnp.bfloat16)
    value_prod = v.astype(jnp.float32) * value_grad.astype(jnp.float32)
    value_terms = [jnp.sum(jnp.where(first, value_prod, 0.0)), jnp.sum(jnp.where(first, 0.0, value_prod))]
    zero_block = jnp.zeros((BLOCK, width), jnp.bfloat16)
    for position in range(WINDOW):
        key_block = zero_block
        value_block = zero_block
        for slot in range(ENC_MOST):
            if 0 <= position - slot <= WINDOW - ENC_MOST:
                rows = slice(slot * BLOCK, (slot + 1) * BLOCK)
                key_block = jnp.where(start == position - slot, key_grad[rows], key_block)
                value_block = jnp.where(start == position - slot, value_grad[rows], value_block)
        grad_refs[position][0] = key_block
        grad_refs[position][1] = value_block
    glane = lax.broadcasted_iota(jnp.int32, gain_ref.shape, 2)
    terms = value_terms + logit_terms
    packed = jnp.zeros(gain_ref.shape, jnp.float32)
    for index, term in enumerate(terms):
        packed = jnp.where(glane == index, term, packed)
    gain_ref[...] = packed


def attention_block(start, head_gains, own, window, allowed_keys):
    _, rows, inner = own.shape
    keys = ENC_MOST * BLOCK
    head_count = head_gains.shape[1]
    width = 2 * (inner // head_count)
    pairs = inner // width
    block_spec = pl.BlockSpec((2, rows, width), lambda i, s, g: (0, 0, i))
    grid_spec = pltpu.PrefetchScalarGridSpec(
        num_scalar_prefetch=2,
        grid=(pairs,),
        in_specs=[block_spec] * (WINDOW + 1) + [pl.BlockSpec((1, keys), lambda i, s, g: (0, 0))],
        out_specs=[block_spec] * (WINDOW + 1) + [pl.BlockSpec((1, 8, 128), lambda i, s, g: (i, 0, 0))],
    )
    flops = 2 * rows * keys * width * 6 * pairs * 2
    cost = pl.CostEstimate(
        flops=flops,
        transcendentals=rows * keys * head_count,
        bytes_accessed=2 * 2 * rows * inner * (2 * WINDOW + 2),
    )
    outs = pl.pallas_call(
        attention_kernel,
        grid_spec=grid_spec,
        out_shape=[jax.ShapeDtypeStruct(own.shape, jnp.bfloat16)] * (WINDOW + 1)
        + [jax.ShapeDtypeStruct((pairs, 8, 128), jnp.float32)],
        cost_estimate=cost,
    )(start, head_gains, own, *window, allowed_keys.astype(jnp.int32)[None, :])
    produced = outs[0]
    grads = tuple(outs[1 : WINDOW + 1])
    packed = outs[WINDOW + 1]
    terms = jnp.stack([packed[:, 0, 0:2].reshape(-1), packed[:, 0, 2:4].reshape(-1)])
    return produced, grads, terms


def group_total(value, axis, size, stride, index):
    count = lax.axis_size(axis)
    gathered = [value]
    for shift in range(1, size):
        pairs = []
        for source in range(count):
            position = (source // stride) % size
            base = source - position * stride
            pairs.append((source, base + ((position - shift) % size) * stride))
        gathered.append(lax.ppermute(value, axis, pairs))
    ordered = jnp.roll(jnp.stack(gathered), (index // stride) % size, axis=0)
    total = ordered[0]
    for position in range(1, size):
        total = total + ordered[position]
    return total


def exchange_add(value, axis, stride):
    count = lax.axis_size(axis)
    return value + lax.ppermute(value, axis, [(i, i ^ stride) for i in range(count)])


def segment_of(block_ids, block_sizes, block_total):
    starts = jnp.cumsum(block_sizes) - block_sizes
    found = jnp.sum((starts[None, :] <= block_ids[:, None]).astype(jnp.int32), axis=1) - 1
    inside = jnp.logical_and(block_ids >= 0, block_ids < block_total)
    return jnp.where(inside, found, -1)


def local_body(sections, head_gains, block_counts):
    phase_index = lax.axis_index("phase")
    shard_index = lax.axis_index("seq")
    count = lax.axis_size("seq")
    local_pair = sections[0]
    tok_dev = local_pair.shape[1]
    head_count = head_gains.shape[1]
    enc_counts = block_counts[0, 0]
    dec_counts = block_counts[0, 1]

    def dec(s):
        return count + s

    def across(value, pairs):
        return lax.ppermute(value, ("phase", "seq"), pairs)

    lower = range(count - 1)
    upper = range(1, count)
    at_home = across(local_pair, [(s, dec(s)) for s in range(count)])
    minus_1 = across(local_pair, [(s + 1, dec(s)) for s in lower])
    plus_1 = across(local_pair, [(s - 1, dec(s)) for s in upper])
    minus_2 = across(minus_1, [(dec(s + 1), dec(s)) for s in lower])
    plus_2 = across(plus_1, [(dec(s - 1), dec(s)) for s in upper])
    minus_3 = across(minus_2, [(dec(s + 1), dec(s)) for s in lower])
    window = [plus_2, plus_1, at_home, minus_1, minus_2, minus_3]

    first_block = shard_index - REACH_LOW
    window_blocks = first_block + jnp.arange(WINDOW, dtype=jnp.int32)
    enc_segs = segment_of(window_blocks, enc_counts, count)
    segment = segment_of(jnp.reshape(shard_index, (1,)), dec_counts, count)[0]
    enc_starts = jnp.cumsum(enc_counts) - enc_counts
    start_block = jnp.clip(enc_starts[segment] - first_block, 0, WINDOW - ENC_MOST).astype(jnp.int32)
    slice_segs = lax.dynamic_slice_in_dim(enc_segs, start_block, ENC_MOST)
    allowed_keys = jnp.repeat(slice_segs == segment, BLOCK)

    def decoder_work(operands):
        own, pieces = operands
        return attention_block(jnp.reshape(start_block, (1,)), head_gains, own, pieces, allowed_keys)

    def encoder_rest(operands):
        own, _ = operands
        zeros = jnp.zeros_like(own)
        return (zeros, (zeros,) * WINDOW, jnp.zeros((2, head_count), jnp.float32))

    produced, grads, terms = lax.cond(
        phase_index == 1, decoder_work, encoder_rest, (local_pair, window)
    )

    def added(a, b):
        return a + b

    token_total = tok_dev * count * lax.axis_size("dp")
    summed = exchange_add(terms, "phase", 1)
    back_minus = across(grads[0], [(dec(s + 1), dec(s)) for s in lower])
    back_plus = across(grads[5], [(dec(s - 1), dec(s)) for s in upper])
    own_sum = across(grads[2], [(dec(s), s) for s in range(count)])
    summed = group_total(summed, "dp", lax.axis_size("dp"), 1, lax.axis_index("dp"))
    summed, back_minus, back_plus = lax.optimization_barrier((summed, back_minus, back_plus))
    minus_sum = across(added(back_minus, grads[1]), [(dec(s + 1), s) for s in lower])
    back_plus = across(added(back_plus, grads[4]), [(dec(s - 1), dec(s)) for s in upper])
    summed = exchange_add(summed, "seq", RING)
    summed, back_plus = lax.optimization_barrier((summed, back_plus))
    plus_sum = across(added(back_plus, grads[3]), [(dec(s - 1), s) for s in upper])
    summed = group_total(summed, "seq", RING, 1, shard_index)
    returned = (
        own_sum.astype(jnp.float32) + minus_sum.astype(jnp.float32) + plus_sum.astype(jnp.float32)
    ).astype(jnp.bfloat16)
    chosen = lax.dynamic_index_in_dim(summed, phase_index, 0, keepdims=False)
    scale = jnp.where(phase_index == 0, head_gains[1], 1.0) * math.sqrt(token_total)
    gain_total = chosen / scale
    result = jnp.where(phase_index == 0, returned, produced)[None]
    return (result, gain_total[None])


def solution(mesh):
    return jax.shard_map(
        local_body,
        mesh=mesh,
        in_specs=(P("phase", None, ("dp", "seq"), None), P(), P("dp", None, None)),
        out_specs=(P("phase", None, ("dp", "seq"), None), P("phase", None)),
        check_vma=False,
    )
```

```python
import math

import jax
import jax.numpy as jnp
from jax import lax
from jax.experimental import pallas as pl
from jax.experimental.pallas import tpu as pltpu
from jax.sharding import PartitionSpec as P


BLOCK = 128
ENC_MOST = 4
REACH_LOW = 2
REACH_HIGH = 3
WINDOW = REACH_LOW + REACH_HIGH + 1
RING = 8

masked_score = -1e30


def attention_kernel(start_ref, gains_ref, own_ref, *refs):
    window_refs = refs[:WINDOW]
    allow_ref = refs[WINDOW]
    out_ref = refs[WINDOW + 1]
    grad_refs = refs[WINDOW + 2 : 2 * WINDOW + 2]
    gain_ref = refs[2 * WINDOW + 2]
    pair = pl.program_id(0)
    start = start_ref[0]
    width = own_ref.shape[2]
    half = width // 2
    inv_root = 1.0 / math.sqrt(half)
    q = own_ref[0]
    do = own_ref[1]
    blocks = [ref[...] for ref in window_refs]

    def pick(slot):
        chosen = blocks[slot + WINDOW - ENC_MOST]
        for shift in range(WINDOW - ENC_MOST - 1, -1, -1):
            chosen = jnp.where(start == shift, blocks[slot + shift], chosen)
        return chosen

    slots = [pick(slot) for slot in range(ENC_MOST)]
    k = jnp.concatenate([piece[0] for piece in slots], axis=0)
    v = jnp.concatenate([piece[1] for piece in slots], axis=0)
    allowed = allow_ref[...] > 0
    rows = q.shape[0]
    lane = lax.broadcasted_iota(jnp.int32, (1, width), 1)
    first = lane < half
    upper_rows = lax.broadcasted_iota(jnp.int32, (2 * rows, 1), 0) < rows
    gl0, gl1 = gains_ref[0, pair * 2], gains_ref[0, pair * 2 + 1]
    gv0, gv1 = gains_ref[1, pair * 2], gains_ref[1, pair * 2 + 1]
    zero_q = jnp.zeros_like(q)
    q2 = jnp.concatenate([jnp.where(first, q, zero_q), jnp.where(first, zero_q, q)], axis=0)
    do2 = jnp.concatenate([jnp.where(first, do, zero_q), jnp.where(first, zero_q, do)], axis=0)
    row_logit = jnp.where(upper_rows, gl0 * inv_root, gl1 * inv_root)
    row_value = jnp.where(upper_rows, gv0, gv1)
    lane_value = jnp.where(first, gv0, gv1)
    lane_factor = jnp.where(first, gl0 * inv_root, gl1 * inv_root)
    raw = lax.dot_general(q2, k, (((1,), (1,)), ((), ())), preferred_element_type=jnp.float32)
    logits = jnp.where(allowed, row_logit * raw, masked_score)
    top = jnp.max(logits, axis=1, keepdims=True)
    lifted = jnp.exp(logits - top)
    chances = lifted * (1.0 / jnp.sum(lifted, axis=1, keepdims=True))
    p_low = chances.astype(jnp.bfloat16)
    pv = jnp.dot(p_low, v, preferred_element_type=jnp.float32)
    attended = jnp.where(first, pv[:rows] * gv0, pv[rows:] * gv1).astype(jnp.bfloat16)
    out_ref[0] = attended
    prod = do.astype(jnp.float32) * attended.astype(jnp.float32)
    carried = jnp.concatenate(
        [jnp.sum(jnp.where(first, prod, 0.0), axis=1, keepdims=True),
         jnp.sum(jnp.where(first, 0.0, prod), axis=1, keepdims=True)],
        axis=0,
    )
    slope = lax.dot_general(do2, v, (((1,), (1,)), ((), ())), preferred_element_type=jnp.float32) * row_value
    score_grad = chances * (slope - carried)
    score_low = score_grad.astype(jnp.bfloat16)
    dq_raw = jnp.dot(score_low, k, preferred_element_type=jnp.float32)
    out_ref[1] = jnp.where(first, dq_raw[:rows] * (gl0 * inv_root), dq_raw[rows:] * (gl1 * inv_root)).astype(jnp.bfloat16)
    key_grad = (
        lax.dot_general(score_low, q2, (((0,), (0,)), ((), ())), preferred_element_type=jnp.float32) * lane_factor
    ).astype(jnp.bfloat16)
    value_grad = (
        lax.dot_general(p_low, do2, (((0,), (0,)), ((), ())), preferred_element_type=jnp.float32) * lane_value
    ).astype(jnp.bfloat16)
    weighted = score_grad * raw
    logit_terms = [jnp.sum(weighted[:rows]) * inv_root, jnp.sum(weighted[rows:]) * inv_root]
    value_prod = v.astype(jnp.float32) * value_grad.astype(jnp.float32)
    value_terms = [jnp.sum(jnp.where(first, value_prod, 0.0)), jnp.sum(jnp.where(first, 0.0, value_prod))]
    zero_block = jnp.zeros((BLOCK, width), jnp.bfloat16)
    for position in range(WINDOW):
        key_block = zero_block
        value_block = zero_block
        for slot in range(ENC_MOST):
            if 0 <= position - slot <= WINDOW - ENC_MOST:
                rows = slice(slot * BLOCK, (slot + 1) * BLOCK)
                key_block = jnp.where(start == position - slot, key_grad[rows], key_block)
                value_block = jnp.where(start == position - slot, value_grad[rows], value_block)
        grad_refs[position][0] = key_block
        grad_refs[position][1] = value_block
    glane = lax.broadcasted_iota(jnp.int32, gain_ref.shape, 2)
    terms = value_terms + logit_terms
    packed = jnp.zeros(gain_ref.shape, jnp.float32)
    for index, term in enumerate(terms):
        packed = jnp.where(glane == index, term, packed)
    gain_ref[...] = packed


def attention_block(start, head_gains, own, window, allowed_keys):
    _, rows, inner = own.shape
    keys = ENC_MOST * BLOCK
    head_count = head_gains.shape[1]
    width = 2 * (inner // head_count)
    pairs = inner // width
    block_spec = pl.BlockSpec((2, rows, width), lambda i, s, g: (0, 0, i))
    grid_spec = pltpu.PrefetchScalarGridSpec(
        num_scalar_prefetch=2,
        grid=(pairs,),
        in_specs=[block_spec] * (WINDOW + 1) + [pl.BlockSpec((1, keys), lambda i, s, g: (0, 0))],
        out_specs=[block_spec] * (WINDOW + 1) + [pl.BlockSpec((1, 8, 128), lambda i, s, g: (i, 0, 0))],
    )
    flops = 2 * rows * keys * width * 6 * pairs * 2
    cost = pl.CostEstimate(
        flops=flops,
        transcendentals=rows * keys * head_count,
        bytes_accessed=2 * 2 * rows * inner * (2 * WINDOW + 2),
    )
    outs = pl.pallas_call(
        attention_kernel,
        grid_spec=grid_spec,
        out_shape=[jax.ShapeDtypeStruct(own.shape, jnp.bfloat16)] * (WINDOW + 1)
        + [jax.ShapeDtypeStruct((pairs, 8, 128), jnp.float32)],
        cost_estimate=cost,
    )(start, head_gains, own, *window, allowed_keys.astype(jnp.int32)[None, :])
    produced = outs[0]
    grads = tuple(outs[1 : WINDOW + 1])
    packed = outs[WINDOW + 1]
    terms = jnp.stack([packed[:, 0, 0:2].reshape(-1), packed[:, 0, 2:4].reshape(-1)])
    return produced, grads, terms


def ring_shift(value, steps):
    count = lax.axis_size("seq")
    pairs = []
    for source in range(count):
        base = source - source % RING
        pairs.append((source, base + (source - steps) % RING))
    return lax.ppermute(value, "seq", pairs)


def ring_total(value, shard_index):
    gathered = value[None]
    gathered = jnp.concatenate([gathered, ring_shift(gathered, 1)], axis=0)
    gathered = jnp.concatenate([gathered, ring_shift(gathered, 2)], axis=0)
    while gathered.shape[0] < RING:
        have = gathered.shape[0]
        gathered = jnp.concatenate([gathered, ring_shift(gathered, 2)[have - 2 : have]], axis=0)
    ordered = jnp.roll(gathered, shard_index % RING, axis=0)
    total = ordered[0]
    for index in range(1, RING):
        total = total + ordered[index]
    return total


def exchange_add(value, axis, stride):
    count = lax.axis_size(axis)
    return value + lax.ppermute(value, axis, [(i, i ^ stride) for i in range(count)])


def segment_of(block_ids, block_sizes, block_total):
    starts = jnp.cumsum(block_sizes) - block_sizes
    found = jnp.sum((starts[None, :] <= block_ids[:, None]).astype(jnp.int32), axis=1) - 1
    inside = jnp.logical_and(block_ids >= 0, block_ids < block_total)
    return jnp.where(inside, found, -1)


def local_body(sections, head_gains, block_counts):
    phase_index = lax.axis_index("phase")
    shard_index = lax.axis_index("seq")
    count = lax.axis_size("seq")
    local_pair = sections[0]
    tok_dev = local_pair.shape[1]
    head_count = head_gains.shape[1]
    enc_counts = block_counts[0, 0]
    dec_counts = block_counts[0, 1]

    def dec(s):
        return count + s

    def across(value, pairs):
        return lax.ppermute(value, ("phase", "seq"), pairs)

    lower = range(count - 1)
    upper = range(1, count)
    at_home = across(local_pair, [(s, dec(s)) for s in range(count)])
    minus_1 = across(local_pair, [(s + 1, dec(s)) for s in lower])
    plus_1 = across(local_pair, [(s - 1, dec(s)) for s in upper])
    minus_2 = across(minus_1, [(dec(s + 1), dec(s)) for s in lower])
    plus_2 = across(plus_1, [(dec(s - 1), dec(s)) for s in upper])
    minus_3 = across(minus_2, [(dec(s + 1), dec(s)) for s in lower])
    window = [plus_2, plus_1, at_home, minus_1, minus_2, minus_3]

    first_block = shard_index - REACH_LOW
    window_blocks = first_block + jnp.arange(WINDOW, dtype=jnp.int32)
    enc_segs = segment_of(window_blocks, enc_counts, count)
    segment = segment_of(jnp.reshape(shard_index, (1,)), dec_counts, count)[0]
    enc_starts = jnp.cumsum(enc_counts) - enc_counts
    start_block = jnp.clip(enc_starts[segment] - first_block, 0, WINDOW - ENC_MOST).astype(jnp.int32)
    slice_segs = lax.dynamic_slice_in_dim(enc_segs, start_block, ENC_MOST)
    allowed_keys = jnp.repeat(slice_segs == segment, BLOCK)

    def decoder_work(operands):
        own, pieces = operands
        return attention_block(jnp.reshape(start_block, (1,)), head_gains, own, pieces, allowed_keys)

    def encoder_rest(operands):
        own, _ = operands
        zeros = jnp.zeros_like(own)
        return (zeros, (zeros,) * WINDOW, jnp.zeros((2, head_count), jnp.float32))

    produced, grads, terms = lax.cond(
        phase_index == 1, decoder_work, encoder_rest, (local_pair, window)
    )

    def added(a, b):
        return a + b

    token_total = tok_dev * count * lax.axis_size("dp")
    summed = exchange_add(terms, "phase", 1)
    back_minus = across(grads[0], [(dec(s + 1), dec(s)) for s in lower])
    back_plus = across(grads[5], [(dec(s - 1), dec(s)) for s in upper])
    own_sum = across(grads[2], [(dec(s), s) for s in range(count)])
    summed = exchange_add(exchange_add(exchange_add(summed, "dp", 1), "dp", 2), "dp", 4)
    summed, back_minus, back_plus = lax.optimization_barrier((summed, back_minus, back_plus))
    minus_sum = across(added(back_minus, grads[1]), [(dec(s + 1), s) for s in lower])
    back_plus = across(added(back_plus, grads[4]), [(dec(s - 1), dec(s)) for s in upper])
    summed = exchange_add(summed, "seq", RING)
    summed, back_plus = lax.optimization_barrier((summed, back_plus))
    plus_sum = across(added(back_plus, grads[3]), [(dec(s - 1), s) for s in upper])
    summed = ring_total(summed, shard_index)
    returned = (
        own_sum.astype(jnp.float32) + minus_sum.astype(jnp.float32) + plus_sum.astype(jnp.float32)
    ).astype(jnp.bfloat16)
    chosen = lax.dynamic_index_in_dim(summed, phase_index, 0, keepdims=False)
    scale = jnp.where(phase_index == 0, head_gains[1], 1.0) * math.sqrt(token_total)
    gain_total = chosen / scale
    result = jnp.where(phase_index == 0, returned, produced)[None]
    return (result, gain_total[None])


def solution(mesh):
    return jax.shard_map(
        local_body,
        mesh=mesh,
        in_specs=(P("phase", None, ("dp", "seq"), None), P(), P("dp", None, None)),
        out_specs=(P("phase", None, ("dp", "seq"), None), P("phase", None)),
        check_vma=False,
    )
```

```python
import math

import jax
import jax.numpy as jnp
from jax import lax
from jax.experimental import pallas as pl
from jax.experimental.pallas import tpu as pltpu
from jax.sharding import PartitionSpec as P


BLOCK = 128
ENC_MOST = 4
REACH_LOW = 2
REACH_HIGH = 3
WINDOW = REACH_LOW + REACH_HIGH + 1
RING = 8
HEADS_PER_STEP = 4

masked_score = -1e30


def attention_kernel(start_ref, gains_ref, own_ref, *refs):
    window_refs = refs[:WINDOW]
    allow_ref = refs[WINDOW]
    out_ref = refs[WINDOW + 1]
    grad_refs = refs[WINDOW + 2 : 2 * WINDOW + 2]
    gain_ref = refs[2 * WINDOW + 2]
    pair = pl.program_id(0)
    start = start_ref[0]
    width = own_ref.shape[2]
    half = width // 2
    inv_root = 1.0 / math.sqrt(half)
    q = own_ref[0]
    do = own_ref[1]
    blocks = [ref[...] for ref in window_refs]

    def pick(slot):
        chosen = blocks[slot + WINDOW - ENC_MOST]
        for shift in range(WINDOW - ENC_MOST - 1, -1, -1):
            chosen = jnp.where(start == shift, blocks[slot + shift], chosen)
        return chosen

    slots = [pick(slot) for slot in range(ENC_MOST)]
    k = jnp.concatenate([piece[0] for piece in slots], axis=0)
    v = jnp.concatenate([piece[1] for piece in slots], axis=0)
    allowed = allow_ref[...] > 0
    rows = q.shape[0]
    size = width // HEADS_PER_STEP
    inv_root = 1.0 / math.sqrt(size)
    lane_head = lax.broadcasted_iota(jnp.int32, (1, width), 1) // size
    row_head = lax.broadcasted_iota(jnp.int32, (HEADS_PER_STEP * rows, 1), 0) // rows
    logit_gains = [gains_ref[0, pair * HEADS_PER_STEP + j] for j in range(HEADS_PER_STEP)]
    value_gains = [gains_ref[1, pair * HEADS_PER_STEP + j] for j in range(HEADS_PER_STEP)]

    def by_head(index, values):
        chosen = values[0]
        for j in range(1, HEADS_PER_STEP):
            chosen = jnp.where(index == j, values[j], chosen)
        return chosen

    zero_q = jnp.zeros_like(q)
    q_stack = jnp.concatenate([jnp.where(lane_head == j, q, zero_q) for j in range(HEADS_PER_STEP)], axis=0)
    do_stack = jnp.concatenate([jnp.where(lane_head == j, do, zero_q) for j in range(HEADS_PER_STEP)], axis=0)
    row_logit = by_head(row_head, [g * inv_root for g in logit_gains])
    row_value = by_head(row_head, value_gains)
    lane_value = by_head(lane_head, value_gains)
    lane_factor = by_head(lane_head, [g * inv_root for g in logit_gains])
    raw = lax.dot_general(q_stack, k, (((1,), (1,)), ((), ())), preferred_element_type=jnp.float32)
    logits = jnp.where(allowed, row_logit * raw, masked_score)
    top = jnp.max(logits, axis=1, keepdims=True)
    lifted = jnp.exp(logits - top)
    chances = lifted * (1.0 / jnp.sum(lifted, axis=1, keepdims=True))
    p_low = chances.astype(jnp.bfloat16)
    pv = jnp.dot(p_low, v, preferred_element_type=jnp.float32)
    attended = by_head(
        lane_head, [pv[j * rows : (j + 1) * rows] * value_gains[j] for j in range(HEADS_PER_STEP)]
    ).astype(jnp.bfloat16)
    out_ref[0] = attended
    prod = do.astype(jnp.float32) * attended.astype(jnp.float32)
    carried = jnp.concatenate(
        [jnp.sum(jnp.where(lane_head == j, prod, 0.0), axis=1, keepdims=True) for j in range(HEADS_PER_STEP)],
        axis=0,
    )
    slope = lax.dot_general(do_stack, v, (((1,), (1,)), ((), ())), preferred_element_type=jnp.float32) * row_value
    score_grad = chances * (slope - carried)
    score_low = score_grad.astype(jnp.bfloat16)
    dq_raw = jnp.dot(score_low, k, preferred_element_type=jnp.float32)
    out_ref[1] = by_head(
        lane_head,
        [dq_raw[j * rows : (j + 1) * rows] * (logit_gains[j] * inv_root) for j in range(HEADS_PER_STEP)],
    ).astype(jnp.bfloat16)
    key_grad = (
        lax.dot_general(score_low, q_stack, (((0,), (0,)), ((), ())), preferred_element_type=jnp.float32) * lane_factor
    ).astype(jnp.bfloat16)
    value_grad = (
        lax.dot_general(p_low, do_stack, (((0,), (0,)), ((), ())), preferred_element_type=jnp.float32) * lane_value
    ).astype(jnp.bfloat16)
    weighted = score_grad * raw
    logit_terms = [jnp.sum(weighted[j * rows : (j + 1) * rows]) * inv_root for j in range(HEADS_PER_STEP)]
    value_prod = v.astype(jnp.float32) * value_grad.astype(jnp.float32)
    value_terms = [jnp.sum(jnp.where(lane_head == j, value_prod, 0.0)) for j in range(HEADS_PER_STEP)]
    zero_block = jnp.zeros((BLOCK, width), jnp.bfloat16)
    for position in range(WINDOW):
        key_block = zero_block
        value_block = zero_block
        for slot in range(ENC_MOST):
            if 0 <= position - slot <= WINDOW - ENC_MOST:
                rows = slice(slot * BLOCK, (slot + 1) * BLOCK)
                key_block = jnp.where(start == position - slot, key_grad[rows], key_block)
                value_block = jnp.where(start == position - slot, value_grad[rows], value_block)
        grad_refs[position][0] = key_block
        grad_refs[position][1] = value_block
    glane = lax.broadcasted_iota(jnp.int32, gain_ref.shape, 2)
    terms = value_terms + logit_terms
    packed = jnp.zeros(gain_ref.shape, jnp.float32)
    for index, term in enumerate(terms):
        packed = jnp.where(glane == index, term, packed)
    gain_ref[...] = packed


def attention_block(start, head_gains, own, window, allowed_keys):
    _, rows, inner = own.shape
    keys = ENC_MOST * BLOCK
    head_count = head_gains.shape[1]
    width = HEADS_PER_STEP * (inner // head_count)
    pairs = inner // width
    block_spec = pl.BlockSpec((2, rows, width), lambda i, s, g: (0, 0, i))
    grid_spec = pltpu.PrefetchScalarGridSpec(
        num_scalar_prefetch=2,
        grid=(pairs,),
        in_specs=[block_spec] * (WINDOW + 1) + [pl.BlockSpec((1, keys), lambda i, s, g: (0, 0))],
        out_specs=[block_spec] * (WINDOW + 1) + [pl.BlockSpec((1, 8, 128), lambda i, s, g: (i, 0, 0))],
    )
    flops = 2 * rows * keys * width * 6 * pairs * 2
    cost = pl.CostEstimate(
        flops=flops,
        transcendentals=rows * keys * head_count,
        bytes_accessed=2 * 2 * rows * inner * (2 * WINDOW + 2),
    )
    outs = pl.pallas_call(
        attention_kernel,
        grid_spec=grid_spec,
        out_shape=[jax.ShapeDtypeStruct(own.shape, jnp.bfloat16)] * (WINDOW + 1)
        + [jax.ShapeDtypeStruct((pairs, 8, 128), jnp.float32)],
        cost_estimate=cost,
    )(start, head_gains, own, *window, allowed_keys.astype(jnp.int32)[None, :])
    produced = outs[0]
    grads = tuple(outs[1 : WINDOW + 1])
    packed = outs[WINDOW + 1]
    terms = jnp.stack(
        [
            packed[:, 0, 0:HEADS_PER_STEP].reshape(-1),
            packed[:, 0, HEADS_PER_STEP : 2 * HEADS_PER_STEP].reshape(-1),
        ]
    )
    return produced, grads, terms


def ring_shift(value, steps):
    count = lax.axis_size("seq")
    pairs = []
    for source in range(count):
        base = source - source % RING
        pairs.append((source, base + (source - steps) % RING))
    return lax.ppermute(value, "seq", pairs)


def ring_total(value, shard_index):
    gathered = value[None]
    gathered = jnp.concatenate([gathered, ring_shift(gathered, 1)], axis=0)
    gathered = jnp.concatenate([gathered, ring_shift(gathered, 2)], axis=0)
    while gathered.shape[0] < RING:
        have = gathered.shape[0]
        gathered = jnp.concatenate([gathered, ring_shift(gathered, 2)[have - 2 : have]], axis=0)
    ordered = jnp.roll(gathered, shard_index % RING, axis=0)
    total = ordered[0]
    for index in range(1, RING):
        total = total + ordered[index]
    return total


def exchange_add(value, axis, stride):
    count = lax.axis_size(axis)
    return value + lax.ppermute(value, axis, [(i, i ^ stride) for i in range(count)])


def segment_of(block_ids, block_sizes, block_total):
    starts = jnp.cumsum(block_sizes) - block_sizes
    found = jnp.sum((starts[None, :] <= block_ids[:, None]).astype(jnp.int32), axis=1) - 1
    inside = jnp.logical_and(block_ids >= 0, block_ids < block_total)
    return jnp.where(inside, found, -1)


def local_body(sections, head_gains, block_counts):
    phase_index = lax.axis_index("phase")
    shard_index = lax.axis_index("seq")
    count = lax.axis_size("seq")
    local_pair = sections[0]
    tok_dev = local_pair.shape[1]
    head_count = head_gains.shape[1]
    enc_counts = block_counts[0, 0]
    dec_counts = block_counts[0, 1]

    def dec(s):
        return count + s

    def across(value, pairs):
        return lax.ppermute(value, ("phase", "seq"), pairs)

    lower = range(count - 1)
    upper = range(1, count)
    at_home = across(local_pair, [(s, dec(s)) for s in range(count)])
    minus_1 = across(local_pair, [(s + 1, dec(s)) for s in lower])
    plus_1 = across(local_pair, [(s - 1, dec(s)) for s in upper])
    minus_2 = across(minus_1, [(dec(s + 1), dec(s)) for s in lower])
    plus_2 = across(plus_1, [(dec(s - 1), dec(s)) for s in upper])
    minus_3 = across(minus_2, [(dec(s + 1), dec(s)) for s in lower])
    window = [plus_2, plus_1, at_home, minus_1, minus_2, minus_3]

    first_block = shard_index - REACH_LOW
    window_blocks = first_block + jnp.arange(WINDOW, dtype=jnp.int32)
    enc_segs = segment_of(window_blocks, enc_counts, count)
    segment = segment_of(jnp.reshape(shard_index, (1,)), dec_counts, count)[0]
    enc_starts = jnp.cumsum(enc_counts) - enc_counts
    start_block = jnp.clip(enc_starts[segment] - first_block, 0, WINDOW - ENC_MOST).astype(jnp.int32)
    slice_segs = lax.dynamic_slice_in_dim(enc_segs, start_block, ENC_MOST)
    allowed_keys = jnp.repeat(slice_segs == segment, BLOCK)

    def decoder_work(operands):
        own, pieces = operands
        return attention_block(jnp.reshape(start_block, (1,)), head_gains, own, pieces, allowed_keys)

    def encoder_rest(operands):
        own, _ = operands
        zeros = jnp.zeros_like(own)
        return (zeros, (zeros,) * WINDOW, jnp.zeros((2, head_count), jnp.float32))

    produced, grads, terms = lax.cond(
        phase_index == 1, decoder_work, encoder_rest, (local_pair, window)
    )

    def added(a, b):
        return a + b

    token_total = tok_dev * count * lax.axis_size("dp")
    summed = exchange_add(terms, "phase", 1)
    back_minus = across(grads[0], [(dec(s + 1), dec(s)) for s in lower])
    back_plus = across(grads[5], [(dec(s - 1), dec(s)) for s in upper])
    own_sum = across(grads[2], [(dec(s), s) for s in range(count)])
    summed = exchange_add(exchange_add(exchange_add(summed, "dp", 1), "dp", 2), "dp", 4)
    summed, back_minus, back_plus = lax.optimization_barrier((summed, back_minus, back_plus))
    minus_sum = across(added(back_minus, grads[1]), [(dec(s + 1), s) for s in lower])
    back_plus = across(added(back_plus, grads[4]), [(dec(s - 1), dec(s)) for s in upper])
    summed = exchange_add(summed, "seq", RING)
    summed, back_plus = lax.optimization_barrier((summed, back_plus))
    plus_sum = across(added(back_plus, grads[3]), [(dec(s - 1), s) for s in upper])
    summed = ring_total(summed, shard_index)
    returned = (
        own_sum.astype(jnp.float32) + minus_sum.astype(jnp.float32) + plus_sum.astype(jnp.float32)
    ).astype(jnp.bfloat16)
    chosen = lax.dynamic_index_in_dim(summed, phase_index, 0, keepdims=False)
    scale = jnp.where(phase_index == 0, head_gains[1], 1.0) * math.sqrt(token_total)
    gain_total = chosen / scale
    result = jnp.where(phase_index == 0, returned, produced)[None]
    return (result, gain_total[None])


def solution(mesh):
    return jax.shard_map(
        local_body,
        mesh=mesh,
        in_specs=(P("phase", None, ("dp", "seq"), None), P(), P("dp", None, None)),
        out_specs=(P("phase", None, ("dp", "seq"), None), P("phase", None)),
        check_vma=False,
    )
```
